32 devices in a mesh: pipe: 8 (over z, y), tensor: 4 (over x, core).
Axes of the slice: x: 2, y: 2, z: 4, core: 2. Of those that a mesh axis runs over, the one named last changes fastest.
Arguments:
- arriving: float32 [8, 8192, 384], P('pipe', 'tensor'), may hold values from -6 to 6
- stash: bfloat16 [2, 8, 8192, 384], P(None, 'pipe', 'tensor'), may hold values from -6 to 6
- grad_in: float32 [8, 8192, 384], P('pipe', 'tensor'), may hold values from -6 to 6
- first_up: bfloat16 [8, 64, 128, 128], P('pipe', 'tensor'), may hold values from -0.5 to 0.5
- second_up: bfloat16 [8, 128, 64, 256], P('pipe', 'tensor'), may hold values from -0.75 to 0.75
- first_down: bfloat16 [8, 128, 64, 256], P('pipe', 'tensor'), may hold values from -0.375 to 0.375
- second_down: bfloat16 [8, 64, 128, 128], P('pipe', 'tensor'), may hold values from -0.5 to 0.5
Outputs:
- arriving_out: float32 [8, 8192, 384], P('pipe', 'tensor')
- grad_out: float32 [8, 8192, 384], P('pipe', 'tensor')
- first_up_grad: float32 [8, 64, 128, 128], P('pipe', 'tensor')
- second_up_grad: float32 [8, 128, 64, 256], P('pipe', 'tensor')
- first_down_grad: float32 [8, 128, 64, 256], P('pipe', 'tensor')
- second_down_grad: float32 [8, 64, 128, 128], P('pipe', 'tensor')
The draws below stay inside these ranges and needn't reach their ends.
All inputs are finite; a program needn't handle non-finite values.
Results may differ from the reference program's by a relative error of at most 0.007.
Values may be sent and summed in bfloat16 or wider, within the bound.
No kernel may reach another device: no remote copies, remote signals or barrier semaphores. Data moves between devices by JAX's collectives and lax.ppermute only.
A program may use at most 192 MiB of HBM per device.

```python
import jax
import jax.numpy as jnp
from jax import lax

D = 8192
BS = 128
ROWS = 384
TICKS = 2
NB = 64
FFB = 256
SECTIONS = 8


def levels(rng, extent, split, smallest, top_value):
    level = 1.0
    for axis_at, parts in split:
        heights = jax.random.uniform(jax.random.fold_in(jax.random.fold_in(rng, 6), axis_at), (parts,), jnp.float32, smallest / len(split), top_value / len(split))
        level = level * jnp.repeat(jnp.exp(heights), extent[axis_at] // parts).reshape((-1,) + (1,) * (len(extent) - 1 - axis_at))
    return level


def normal_values(own_key, dims, spread, bound, shards=(), dtype=jnp.bfloat16):
    values = spread * jax.random.normal(own_key, dims, jnp.float32)
    if shards:
        values = values * levels(own_key, dims, shards, -0.22, 0.18)
    return jnp.clip(values, -bound, bound).astype(dtype)


def setup_inputs(seed: int = 0) -> dict:
    arg_keys = jax.random.split(jax.random.key(seed), 8)
    return {
        "arriving": normal_values(arg_keys[0], (SECTIONS, D, ROWS), 1.0, 6.0, ((0, 8), (1, 4)), jnp.float32),
        "stash": normal_values(arg_keys[1], (TICKS, SECTIONS, D, ROWS), 1.0, 6.0, ((1, 8), (2, 4))),
        "grad_in": normal_values(arg_keys[2], (SECTIONS, D, ROWS), 1.0, 6.0, ((0, 8), (1, 4)), jnp.float32),
        "first_up": normal_values(arg_keys[3], (SECTIONS, NB, BS, BS), BS ** -0.5, 0.5, ((0, 8), (1, 4))),
        "second_up": normal_values(arg_keys[4], (SECTIONS, BS, NB, FFB), NB ** -0.5, 0.75, ((0, 8), (1, 4))),
        "first_down": normal_values(arg_keys[5], (SECTIONS, BS, NB, FFB), FFB ** -0.5, 0.375, ((0, 8), (1, 4))),
        "second_down": normal_values(arg_keys[6], (SECTIONS, NB, BS, BS), BS ** -0.5, 0.5, ((0, 8), (1, 4))),
    }


def smooth(values):
    return jax.nn.gelu(values, approximate=True)

def front(narrow_in, first_up, second_up, first_down):
    first_out = jnp.einsum('njr,nji->nir', narrow_in.astype(jnp.float32), first_up.astype(jnp.float32)).astype(jnp.bfloat16)
    hidden_pre = jnp.einsum('nir,inf->ifr', first_out.astype(jnp.float32), second_up.astype(jnp.float32))
    hidden = smooth(hidden_pre).astype(jnp.bfloat16)
    folded = jnp.einsum('ifr,inf->nir', hidden.astype(jnp.float32), first_down.astype(jnp.float32)).astype(jnp.bfloat16)
    return (first_out, hidden_pre, hidden, folded)

def section(activation, stored, cotangent, first_up, second_up, first_down, second_down):
    blocks = first_up.shape[0]
    width = first_up.shape[1]
    rows = activation.shape[1]
    current = activation.astype(jnp.bfloat16).reshape(blocks, width, rows)
    folded_ahead = front(current, first_up, second_up, first_down)[3]
    output = activation + jnp.einsum('nir,nik->nkr', folded_ahead.astype(jnp.float32), second_down.astype(jnp.float32)).reshape(activation.shape)
    narrow_in = stored.reshape(blocks, width, rows)
    first_out, hidden_pre, hidden, folded = front(narrow_in, first_up, second_up, first_down)
    narrow_grad = cotangent.astype(jnp.bfloat16).reshape(blocks, width, rows)
    grad_second_down = jnp.einsum('nir,nkr->nik', folded.astype(jnp.float32), narrow_grad.astype(jnp.float32))
    grad_folded = jnp.einsum('nkr,nik->nir', narrow_grad.astype(jnp.float32), second_down.astype(jnp.float32)).astype(jnp.bfloat16)
    grad_first_down = jnp.einsum('ifr,nir->inf', hidden.astype(jnp.float32), grad_folded.astype(jnp.float32))
    grad_hidden = jnp.einsum('nir,inf->ifr', grad_folded.astype(jnp.float32), first_down.astype(jnp.float32))
    smooth_back = jax.vjp(smooth, hidden_pre)[1]
    grad_pre = smooth_back(grad_hidden)[0].astype(jnp.bfloat16)
    grad_second_up = jnp.einsum('nir,ifr->inf', first_out.astype(jnp.float32), grad_pre.astype(jnp.float32))
    grad_first = jnp.einsum('ifr,inf->nir', grad_pre.astype(jnp.float32), second_up.astype(jnp.float32)).astype(jnp.bfloat16)
    grad_first_up = jnp.einsum('njr,nir->nji', narrow_in.astype(jnp.float32), grad_first.astype(jnp.float32))
    grad_input = cotangent + jnp.einsum('nir,nji->njr', grad_first.astype(jnp.float32), first_up.astype(jnp.float32)).reshape(cotangent.shape)
    return (output, grad_input, grad_first_up, grad_second_up, grad_first_down, grad_second_down)

def apply_section(item):
    return section(*item)

def reference(arriving, stash, grad_in, first_up, second_up, first_down, second_down):
    activation = arriving
    cotangent = grad_in
    totals = [jnp.zeros(first_up.shape, jnp.float32), jnp.zeros(second_up.shape, jnp.float32), jnp.zeros(first_down.shape, jnp.float32), jnp.zeros(second_down.shape, jnp.float32)]
    for position in range(TICKS):
        result = lax.map(apply_section, (activation, stash[position], cotangent, first_up, second_up, first_down, second_down))
        activation = jnp.roll(result[0], 1, axis=0)
        cotangent = jnp.roll(result[1], -1, axis=0)
        totals = [totals[0] + result[2], totals[1] + result[3], totals[2] + result[4], totals[3] + result[5]]
    return (activation, cotangent, totals[0], totals[1], totals[2], totals[3])
```

```python
import jax
import jax.numpy as jnp
from jax import lax
from jax.sharding import PartitionSpec as P


def shifted(value, axis, by):
    count = lax.axis_size(axis)
    return lax.ppermute(value, axis, [(i, (i + by) % count) for i in range(count)])


def smooth(values):
    return jax.nn.gelu(values, approximate=True)


def to_columns(value):
    return lax.all_to_all(value, "tensor", split_axis=1, concat_axis=0, tiled=True)


def to_rows(value):
    return lax.all_to_all(value, "tensor", split_axis=0, concat_axis=1, tiled=True)


def front(narrow_in, first_up, second_up, first_down):
    first_out = jnp.einsum(
        "njr,nji->nir", narrow_in, first_up, preferred_element_type=jnp.float32
    ).astype(jnp.bfloat16)
    spread = to_columns(first_out)
    hidden_pre = jnp.einsum("nir,inf->ifr", spread, second_up, preferred_element_type=jnp.float32)
    hidden = smooth(hidden_pre).astype(jnp.bfloat16)
    local_fold = jnp.einsum(
        "ifr,inf->nir", hidden, first_down, preferred_element_type=jnp.float32
    ).astype(jnp.bfloat16)
    folded = to_rows(local_fold)
    return (spread, hidden_pre, hidden, folded)


def backward(narrow_in, cotangent, first_up, second_up, first_down, second_down, parts):
    spread, hidden_pre, hidden, folded = parts
    narrow_grad = cotangent.astype(jnp.bfloat16).reshape(narrow_in.shape)
    grad_second_down = jnp.einsum(
        "nir,nkr->nik", folded, narrow_grad, preferred_element_type=jnp.float32
    )
    local_grad = jnp.einsum(
        "nkr,nik->nir", narrow_grad, second_down, preferred_element_type=jnp.float32
    ).astype(jnp.bfloat16)
    grad_folded = to_columns(local_grad)
    grad_first_down = jnp.einsum(
        "ifr,nir->inf", hidden, grad_folded, preferred_element_type=jnp.float32
    )
    grad_hidden = jnp.einsum(
        "nir,inf->ifr", grad_folded, first_down, preferred_element_type=jnp.float32
    )
    smooth_back = jax.vjp(smooth, hidden_pre)[1]
    grad_pre = smooth_back(grad_hidden)[0].astype(jnp.bfloat16)
    grad_second_up = jnp.einsum(
        "nir,ifr->inf", spread, grad_pre, preferred_element_type=jnp.float32
    )
    column_grad = jnp.einsum(
        "ifr,inf->nir", grad_pre, second_up, preferred_element_type=jnp.float32
    ).astype(jnp.bfloat16)
    grad_first = to_rows(column_grad)
    grad_first_up = jnp.einsum(
        "njr,nir->nji", narrow_in, grad_first, preferred_element_type=jnp.float32
    )
    grad_input = jnp.einsum(
        "nir,nji->njr", grad_first, first_up, preferred_element_type=jnp.float32
    ).reshape(cotangent.shape)
    return (grad_input, (grad_first_up, grad_second_up, grad_first_down, grad_second_down))


def body(arriving, stash, grad_in, first_up, second_up, first_down, second_down):
    activation = arriving[0]
    cotangent = grad_in[0]
    up_first = first_up[0]
    up_second = second_up[0]
    down_first = first_down[0]
    down_second = second_down[0]
    blocks = up_first.shape[0]
    width = up_first.shape[1]
    rows = activation.shape[1]
    stored = stash[0, 0].reshape(blocks, width, rows)
    current = activation.astype(jnp.bfloat16).reshape(blocks, width, rows)
    folded_ahead = front(current, up_first, up_second, down_first)[3]
    behind = front(stored, up_first, up_second, down_first)
    output = activation + jnp.einsum(
        "nir,nik->nkr", folded_ahead, down_second, preferred_element_type=jnp.float32
    ).reshape(activation.shape)
    grad_input, terms = backward(
        stored, cotangent, up_first, up_second, down_first, down_second, behind
    )
    grad_input = cotangent + grad_input
    totals = terms
    near_activation = shifted(output.astype(jnp.bfloat16), "pipe", 1)
    near_cotangent = shifted(grad_input.astype(jnp.bfloat16), "pipe", -1)
    far_activation = shifted(output, "pipe", 2)
    far_cotangent = shifted(grad_input, "pipe", -2)

    stored = stash[1, 0].reshape(blocks, width, rows)
    current = near_activation.reshape(blocks, width, rows)
    folded_ahead = front(current, up_first, up_second, down_first)[3]
    behind = front(stored, up_first, up_second, down_first)
    step = jnp.einsum(
        "nir,nik->nkr", folded_ahead, down_second, preferred_element_type=jnp.float32
    ).reshape(activation.shape)
    grad_step, terms = backward(
        stored, near_cotangent, up_first, up_second, down_first, down_second, behind
    )
    activation = far_activation + shifted(step.astype(jnp.bfloat16), "pipe", 1)
    cotangent = far_cotangent + shifted(grad_step.astype(jnp.bfloat16), "pipe", -1)
    totals = (
        totals[0] + terms[0],
        totals[1] + terms[1],
        totals[2] + terms[2],
        totals[3] + terms[3],
    )
    return (
        activation[None],
        cotangent[None],
        totals[0][None],
        totals[1][None],
        totals[2][None],
        totals[3][None],
    )


def solution(mesh):
    placed = (
        P("pipe", "tensor", None),
        P(None, "pipe", "tensor", None),
        P("pipe", "tensor", None),
        P("pipe", "tensor", None, None),
        P("pipe", "tensor", None, None),
        P("pipe", "tensor", None, None),
        P("pipe", "tensor", None, None),
    )
    return jax.shard_map(
        body,
        mesh=mesh,
        in_specs=placed,
        out_specs=(
            P("pipe", "tensor", None),
            P("pipe", "tensor", None),
            P("pipe", "tensor", None, None),
            P("pipe", "tensor", None, None),
            P("pipe", "tensor", None, None),
            P("pipe", "tensor", None, None),
        ),
        check_vma=False,
    )
```

```python
import jax
import jax.numpy as jnp
from jax import lax
from jax.sharding import PartitionSpec as P


def shifted(value, axis, by):
    count = lax.axis_size(axis)
    return lax.ppermute(value, axis, [(i, (i + by) % count) for i in range(count)])


def smooth(values):
    return jax.nn.gelu(values, approximate=True)


def to_columns(value):
    return lax.all_to_all(value, "tensor", split_axis=1, concat_axis=0, tiled=True)


def to_rows(value):
    return lax.all_to_all(value, "tensor", split_axis=0, concat_axis=1, tiled=True)


def front(narrow_in, first_up, second_up, first_down):
    first_out = jnp.einsum(
        "njr,nji->nir", narrow_in, first_up, preferred_element_type=jnp.float32
    ).astype(jnp.bfloat16)
    spread = to_columns(first_out)
    hidden_pre = jnp.einsum("nir,inf->ifr", spread, second_up, preferred_element_type=jnp.float32)
    hidden = smooth(hidden_pre).astype(jnp.bfloat16)
    local_fold = jnp.einsum(
        "ifr,inf->nir", hidden, first_down, preferred_element_type=jnp.float32
    ).astype(jnp.bfloat16)
    folded = to_rows(local_fold)
    return (spread, hidden_pre, hidden, folded)


def backward(narrow_in, cotangent, first_up, second_up, first_down, second_down, parts):
    spread, hidden_pre, hidden, folded = parts
    narrow_grad = cotangent.astype(jnp.bfloat16).reshape(narrow_in.shape)
    grad_second_down = jnp.einsum(
        "nir,nkr->nik", folded, narrow_grad, preferred_element_type=jnp.float32
    )
    local_grad = jnp.einsum(
        "nkr,nik->nir", narrow_grad, second_down, preferred_element_type=jnp.float32
    ).astype(jnp.bfloat16)
    grad_folded = to_columns(local_grad)
    grad_first_down = jnp.einsum(
        "ifr,nir->inf", hidden, grad_folded, preferred_element_type=jnp.float32
    )
    grad_hidden = jnp.einsum(
        "nir,inf->ifr", grad_folded, first_down, preferred_element_type=jnp.float32
    )
    smooth_back = jax.vjp(smooth, hidden_pre)[1]
    grad_pre = smooth_back(grad_hidden)[0].astype(jnp.bfloat16)
    grad_second_up = jnp.einsum(
        "nir,ifr->inf", spread, grad_pre, preferred_element_type=jnp.float32
    )
    column_grad = jnp.einsum(
        "ifr,inf->nir", grad_pre, second_up, preferred_element_type=jnp.float32
    ).astype(jnp.bfloat16)
    grad_first = to_rows(column_grad)
    grad_first_up = jnp.einsum(
        "njr,nir->nji", narrow_in, grad_first, preferred_element_type=jnp.float32
    )
    grad_input = jnp.einsum(
        "nir,nji->njr", grad_first, first_up, preferred_element_type=jnp.float32
    ).reshape(cotangent.shape)
    return (grad_input, (grad_first_up, grad_second_up, grad_first_down, grad_second_down))


def body(arriving, stash, grad_in, first_up, second_up, first_down, second_down):
    activation = arriving[0]
    cotangent = grad_in[0]
    up_first = first_up[0]
    up_second = second_up[0]
    down_first = first_down[0]
    down_second = second_down[0]
    blocks = up_first.shape[0]
    width = up_first.shape[1]
    rows = activation.shape[1]
    far_activation = shifted(activation, "pipe", 2)
    far_cotangent = shifted(cotangent, "pipe", -2)

    current = activation.astype(jnp.bfloat16).reshape(blocks, width, rows)
    folded_ahead = front(current, up_first, up_second, down_first)[3]
    step = jnp.einsum(
        "nir,nik->nkr", folded_ahead, down_second, preferred_element_type=jnp.float32
    ).reshape(activation.shape)
    output = activation + step
    near_activation = shifted(output.astype(jnp.bfloat16), "pipe", 1)
    step, cotangent = lax.optimization_barrier((step, cotangent))

    stored = stash[0, 0].reshape(blocks, width, rows)
    behind = front(stored, up_first, up_second, down_first)
    grad_step, totals = backward(
        stored, cotangent, up_first, up_second, down_first, down_second, behind
    )
    grad_input = cotangent + grad_step
    near_cotangent = shifted(grad_input.astype(jnp.bfloat16), "pipe", -1)
    step, grad_step, far_activation, far_cotangent = lax.optimization_barrier(
        (step, grad_step, far_activation, far_cotangent)
    )
    far_step = shifted(step.astype(jnp.bfloat16), "pipe", 2)
    far_grad_step = shifted(grad_step.astype(jnp.bfloat16), "pipe", -2)

    current = near_activation.reshape(blocks, width, rows)
    folded_ahead = front(current, up_first, up_second, down_first)[3]
    step = jnp.einsum(
        "nir,nik->nkr", folded_ahead, down_second, preferred_element_type=jnp.float32
    ).reshape(activation.shape)
    last_step = shifted(step.astype(jnp.bfloat16), "pipe", 1)
    step, near_cotangent, far_step, far_grad_step = lax.optimization_barrier(
        (step, near_cotangent, far_step, far_grad_step)
    )

    stored = stash[1, 0].reshape(blocks, width, rows)
    behind = front(stored, up_first, up_second, down_first)
    grad_step, terms = backward(
        stored, near_cotangent, up_first, up_second, down_first, down_second, behind
    )
    last_grad_step = shifted(grad_step.astype(jnp.bfloat16), "pipe", -1)
    activation = far_activation + (
        far_step.astype(jnp.float32) + last_step.astype(jnp.float32)
    )
    cotangent = far_cotangent + (
        far_grad_step.astype(jnp.float32) + last_grad_step.astype(jnp.float32)
    )
    totals = (
        totals[0] + terms[0],
        totals[1] + terms[1],
        totals[2] + terms[2],
        totals[3] + terms[3],
    )
    return (
        activation[None],
        cotangent[None],
        totals[0][None],
        totals[1][None],
        totals[2][None],
        totals[3][None],
    )


def solution(mesh):
    placed = (
        P("pipe", "tensor", None),
        P(None, "pipe", "tensor", None),
        P("pipe", "tensor", None),
        P("pipe", "tensor", None, None),
        P("pipe", "tensor", None, None),
        P("pipe", "tensor", None, None),
        P("pipe", "tensor", None, None),
    )
    return jax.shard_map(
        body,
        mesh=mesh,
        in_specs=placed,
        out_specs=(
            P("pipe", "tensor", None),
            P("pipe", "tensor", None),
            P("pipe", "tensor", None, None),
            P("pipe", "tensor", None, None),
            P("pipe", "tensor", None, None),
            P("pipe", "tensor", None, None),
        ),
        check_vma=False,
    )
```

```python
import jax
import jax.numpy as jnp
from jax import lax
from jax.sharding import PartitionSpec as P


def shifted(value, axis, by):
    count = lax.axis_size(axis)
    return lax.ppermute(value, axis, [(i, (i + by) % count) for i in range(count)])


def smooth(values):
    return jax.nn.gelu(values, approximate=True)


def to_columns(value):
    return lax.all_to_all(value, "tensor", split_axis=1, concat_axis=0, tiled=True)


def to_rows(value):
    return lax.all_to_all(value, "tensor", split_axis=0, concat_axis=1, tiled=True)


def front(narrow_in, first_up, second_up, first_down):
    first_out = jnp.einsum(
        "njr,nji->nir", narrow_in, first_up, preferred_element_type=jnp.float32
    ).astype(jnp.bfloat16)
    spread = to_columns(first_out)
    hidden_pre = jnp.einsum("nir,inf->ifr", spread, second_up, preferred_element_type=jnp.float32)
    hidden = smooth(hidden_pre).astype(jnp.bfloat16)
    local_fold = jnp.einsum(
        "ifr,inf->nir", hidden, first_down, preferred_element_type=jnp.float32
    ).astype(jnp.bfloat16)
    folded = to_rows(local_fold)
    return (spread, hidden_pre, hidden, folded)


def backward(narrow_in, cotangent, first_up, second_up, first_down, second_down, parts):
    spread, hidden_pre, hidden, folded = parts
    narrow_grad = cotangent.astype(jnp.bfloat16).reshape(narrow_in.shape)
    grad_second_down = jnp.einsum(
        "nir,nkr->nik", folded, narrow_grad, preferred_element_type=jnp.float32
    )
    local_grad = jnp.einsum(
        "nkr,nik->nir", narrow_grad, second_down, preferred_element_type=jnp.float32
    ).astype(jnp.bfloat16)
    grad_folded = to_columns(local_grad)
    grad_first_down = jnp.einsum(
        "ifr,nir->inf", hidden, grad_folded, preferred_element_type=jnp.float32
    )
    grad_hidden = jnp.einsum(
        "nir,inf->ifr", grad_folded, first_down, preferred_element_type=jnp.float32
    )
    smooth_back = jax.vjp(smooth, hidden_pre)[1]
    grad_pre = smooth_back(grad_hidden)[0].astype(jnp.bfloat16)
    grad_second_up = jnp.einsum(
        "nir,ifr->inf", spread, grad_pre, preferred_element_type=jnp.float32
    )
    column_grad = jnp.einsum(
        "ifr,inf->nir", grad_pre, second_up, preferred_element_type=jnp.float32
    ).astype(jnp.bfloat16)
    grad_first = to_rows(column_grad)
    grad_first_up = jnp.einsum(
        "njr,nir->nji", narrow_in, grad_first, preferred_element_type=jnp.float32
    )
    grad_input = jnp.einsum(
        "nir,nji->njr", grad_first, first_up, preferred_element_type=jnp.float32
    ).reshape(cotangent.shape)
    return (grad_input, (grad_first_up, grad_second_up, grad_first_down, grad_second_down))


def body(arriving, stash, grad_in, first_up, second_up, first_down, second_down):
    activation = arriving[0]
    cotangent = grad_in[0]
    up_first = first_up[0]
    up_second = second_up[0]
    down_first = first_down[0]
    down_second = second_down[0]
    blocks = up_first.shape[0]
    width = up_first.shape[1]
    rows = activation.shape[1]
    current = activation.astype(jnp.bfloat16)
    folded_ahead = front(current.reshape(blocks, width, rows), up_first, up_second, down_first)[3]
    output = activation + jnp.einsum(
        "nir,nik->nkr", folded_ahead, down_second, preferred_element_type=jnp.float32
    ).reshape(activation.shape)
    sent = output.astype(jnp.bfloat16)
    near_activation = shifted(sent, "pipe", 1)
    sent, cotangent = lax.optimization_barrier((sent, cotangent))

    stored = stash[0, 0].reshape(blocks, width, rows)
    behind = front(stored, up_first, up_second, down_first)
    grad_step, totals = backward(
        stored, cotangent, up_first, up_second, down_first, down_second, behind
    )
    sent_back = (cotangent + grad_step).astype(jnp.bfloat16)
    near_cotangent = shifted(sent_back, "pipe", -1)
    near_activation, sent_back = lax.optimization_barrier((near_activation, sent_back))

    folded_ahead = front(near_activation.reshape(blocks, width, rows), up_first, up_second, down_first)[3]
    output = near_activation.astype(jnp.float32) + jnp.einsum(
        "nir,nik->nkr", folded_ahead, down_second, preferred_element_type=jnp.float32
    ).reshape(activation.shape)
    sent = output.astype(jnp.bfloat16)
    last_activation = shifted(sent, "pipe", 1)
    sent, near_cotangent = lax.optimization_barrier((sent, near_cotangent))

    stored = stash[1, 0].reshape(blocks, width, rows)
    behind = front(stored, up_first, up_second, down_first)
    grad_step, terms = backward(
        stored, near_cotangent, up_first, up_second, down_first, down_second, behind
    )
    sent_back = (near_cotangent.astype(jnp.float32) + grad_step).astype(jnp.bfloat16)
    last_cotangent = shifted(sent_back, "pipe", -1)
    activation = last_activation.astype(jnp.float32)
    cotangent = last_cotangent.astype(jnp.float32)
    totals = (
        totals[0] + terms[0],
        totals[1] + terms[1],
        totals[2] + terms[2],
        totals[3] + terms[3],
    )
    return (
        activation[None],
        cotangent[None],
        totals[0][None],
        totals[1][None],
        totals[2][None],
        totals[3][None],
    )


def solution(mesh):
    placed = (
        P("pipe", "tensor", None),
        P(None, "pipe", "tensor", None),
        P("pipe", "tensor", None),
        P("pipe", "tensor", None, None),
        P("pipe", "tensor", None, None),
        P("pipe", "tensor", None, None),
        P("pipe", "tensor", None, None),
    )
    return jax.shard_map(
        body,
        mesh=mesh,
        in_specs=placed,
        out_specs=(
            P("pipe", "tensor", None),
            P("pipe", "tensor", None),
            P("pipe", "tensor", None, None),
            P("pipe", "tensor", None, None),
            P("pipe", "tensor", None, None),
            P("pipe", "tensor", None, None),
        ),
        check_vma=False,
    )
```

```python
import jax
import jax.numpy as jnp
from jax import lax
from jax.sharding import PartitionSpec as P


def shifted(value, axis, by):
    count = lax.axis_size(axis)
    return lax.ppermute(value, axis, [(i, (i + by) % count) for i in range(count)])


def smooth(values):
    return jax.nn.gelu(values, approximate=True)


def to_columns(value):
    return lax.all_to_all(value, "tensor", split_axis=1, concat_axis=0, tiled=True)


def to_rows(value):
    return lax.all_to_all(value, "tensor", split_axis=0, concat_axis=1, tiled=True)


def front(narrow_in, first_up, second_up, first_down):
    first_out = jnp.einsum(
        "njr,nji->nir", narrow_in, first_up, preferred_element_type=jnp.float32
    ).astype(jnp.bfloat16)
    spread = to_columns(first_out)
    hidden_pre = jnp.einsum("nir,inf->ifr", spread, second_up, preferred_element_type=jnp.float32)
    hidden = smooth(hidden_pre).astype(jnp.bfloat16)
    local_fold = jnp.einsum(
        "ifr,inf->nir", hidden, first_down, preferred_element_type=jnp.float32
    ).astype(jnp.bfloat16)
    folded = to_rows(local_fold)
    return (spread, hidden_pre, hidden, folded)


def backward(narrow_in, cotangent, first_up, second_up, first_down, second_down, parts):
    spread, hidden_pre, hidden, folded = parts
    narrow_grad = cotangent.astype(jnp.bfloat16).reshape(narrow_in.shape)
    grad_second_down = jnp.einsum(
        "nir,nkr->nik", folded, narrow_grad, preferred_element_type=jnp.float32
    )
    local_grad = jnp.einsum(
        "nkr,nik->nir", narrow_grad, second_down, preferred_element_type=jnp.float32
    ).astype(jnp.bfloat16)
    grad_folded = to_columns(local_grad)
    grad_first_down = jnp.einsum(
        "ifr,nir->inf", hidden, grad_folded, preferred_element_type=jnp.float32
    )
    grad_hidden = jnp.einsum(
        "nir,inf->ifr", grad_folded, first_down, preferred_element_type=jnp.float32
    )
    smooth_back = jax.vjp(smooth, hidden_pre)[1]
    grad_pre = smooth_back(grad_hidden)[0].astype(jnp.bfloat16)
    grad_second_up = jnp.einsum(
        "nir,ifr->inf", spread, grad_pre, preferred_element_type=jnp.float32
    )
    column_grad = jnp.einsum(
        "ifr,inf->nir", grad_pre, second_up, preferred_element_type=jnp.float32
    ).astype(jnp.bfloat16)
    grad_first = to_rows(column_grad)
    grad_first_up = jnp.einsum(
        "njr,nir->nji", narrow_in, grad_first, preferred_element_type=jnp.float32
    )
    grad_input = jnp.einsum(
        "nir,nji->njr", grad_first, first_up, preferred_element_type=jnp.float32
    ).reshape(cotangent.shape)
    return (grad_input, (grad_first_up, grad_second_up, grad_first_down, grad_second_down))


def body(arriving, stash, grad_in, first_up, second_up, first_down, second_down):
    activation = arriving[0]
    cotangent = grad_in[0]
    up_first = first_up[0]
    up_second = second_up[0]
    down_first = first_down[0]
    down_second = second_down[0]
    blocks = up_first.shape[0]
    width = up_first.shape[1]
    rows = activation.shape[1]
    joined = jnp.concatenate(
        [activation.astype(jnp.bfloat16), stash[0, 0], stash[1, 0]], axis=-1
    ).reshape(blocks, width, 3 * rows)
    fronts = front(joined, up_first, up_second, down_first)

    def part(index):
        return tuple(value[..., index * rows:(index + 1) * rows] for value in fronts)

    folded_ahead = part(0)[3]
    output = activation + jnp.einsum(
        "nir,nik->nkr", folded_ahead, down_second, preferred_element_type=jnp.float32
    ).reshape(activation.shape)
    sent = output.astype(jnp.bfloat16)
    near_activation = shifted(sent, "pipe", 1)
    sent, cotangent = lax.optimization_barrier((sent, cotangent))

    stored = stash[0, 0].reshape(blocks, width, rows)
    grad_step, totals = backward(
        stored, cotangent, up_first, up_second, down_first, down_second, part(1)
    )
    sent_back = (cotangent + grad_step).astype(jnp.bfloat16)
    near_cotangent = shifted(sent_back, "pipe", -1)
    near_activation, sent_back = lax.optimization_barrier((near_activation, sent_back))

    folded_ahead = front(near_activation.reshape(blocks, width, rows), up_first, up_second, down_first)[3]
    output = near_activation.astype(jnp.float32) + jnp.einsum(
        "nir,nik->nkr", folded_ahead, down_second, preferred_element_type=jnp.float32
    ).reshape(activation.shape)
    sent = output.astype(jnp.bfloat16)
    last_activation = shifted(sent, "pipe", 1)
    sent, near_cotangent = lax.optimization_barrier((sent, near_cotangent))

    stored = stash[1, 0].reshape(blocks, width, rows)
    grad_step, terms = backward(
        stored, near_cotangent, up_first, up_second, down_first, down_second, part(2)
    )
    sent_back = (near_cotangent.astype(jnp.float32) + grad_step).astype(jnp.bfloat16)
    last_cotangent = shifted(sent_back, "pipe", -1)
    activation = last_activation.astype(jnp.float32)
    cotangent = last_cotangent.astype(jnp.float32)
    totals = (
        totals[0] + terms[0],
        totals[1] + terms[1],
        totals[2] + terms[2],
        totals[3] + terms[3],
    )
    return (
        activation[None],
        cotangent[None],
        totals[0][None],
        totals[1][None],
        totals[2][None],
        totals[3][None],
    )


def solution(mesh):
    placed = (
        P("pipe", "tensor", None),
        P(None, "pipe", "tensor", None),
        P("pipe", "tensor", None),
        P("pipe", "tensor", None, None),
        P("pipe", "tensor", None, None),
        P("pipe", "tensor", None, None),
        P("pipe", "tensor", None, None),
    )
    return jax.shard_map(
        body,
        mesh=mesh,
        in_specs=placed,
        out_specs=(
            P("pipe", "tensor", None),
            P("pipe", "tensor", None),
            P("pipe", "tensor", None, None),
            P("pipe", "tensor", None, None),
            P("pipe", "tensor", None, None),
            P("pipe", "tensor", None, None),
        ),
        check_vma=False,
    )
```

```python
import jax
import jax.numpy as jnp
from jax import lax
from jax.sharding import PartitionSpec as P


def shifted(value, axis, by):
    count = lax.axis_size(axis)
    return lax.ppermute(value, axis, [(i, (i + by) % count) for i in range(count)])


def smooth(values):
    return jax.nn.gelu(values, approximate=True)


def to_columns(value):
    return lax.all_to_all(value, "tensor", split_axis=1, concat_axis=0, tiled=True)


def to_rows(value):
    return lax.all_to_all(value, "tensor", split_axis=0, concat_axis=1, tiled=True)


def front(narrow_in, first_up, second_up, first_down):
    first_out = jnp.einsum(
        "njr,nji->nir", narrow_in, first_up, preferred_element_type=jnp.float32
    ).astype(jnp.bfloat16)
    spread = to_columns(first_out)
    hidden_pre = jnp.einsum("nir,inf->ifr", spread, second_up, preferred_element_type=jnp.float32)
    hidden = smooth(hidden_pre).astype(jnp.bfloat16)
    local_fold = jnp.einsum(
        "ifr,inf->nir", hidden, first_down, preferred_element_type=jnp.float32
    ).astype(jnp.bfloat16)
    folded = to_rows(local_fold)
    return (spread, hidden_pre, hidden, folded)


def backward(narrow_in, cotangent, first_up, second_up, first_down, second_down, parts, held=None):
    spread, hidden_pre, hidden, folded = parts
    narrow_grad = cotangent.astype(jnp.bfloat16).reshape(narrow_in.shape)
    grad_second_down = jnp.einsum(
        "nir,nkr->nik", folded, narrow_grad, preferred_element_type=jnp.float32
    )
    local_grad = jnp.einsum(
        "nkr,nik->nir", narrow_grad, second_down, preferred_element_type=jnp.float32
    ).astype(jnp.bfloat16)
    grad_folded = to_columns(local_grad)
    grad_first_down = jnp.einsum(
        "ifr,nir->inf", hidden, grad_folded, preferred_element_type=jnp.float32
    )
    grad_hidden = jnp.einsum(
        "nir,inf->ifr", grad_folded, first_down, preferred_element_type=jnp.float32
    )
    smooth_back = jax.vjp(smooth, hidden_pre)[1]
    grad_pre = smooth_back(grad_hidden)[0].astype(jnp.bfloat16)
    grad_second_up = jnp.einsum(
        "nir,ifr->inf", spread, grad_pre, preferred_element_type=jnp.float32
    )
    column_grad = jnp.einsum(
        "ifr,inf->nir", grad_pre, second_up, preferred_element_type=jnp.float32
    ).astype(jnp.bfloat16)
    if held is not None:
        column_grad, held = lax.optimization_barrier((column_grad, held))
    grad_first = to_rows(column_grad)
    grad_first_up = jnp.einsum(
        "njr,nir->nji", narrow_in, grad_first, preferred_element_type=jnp.float32
    )
    grad_input = jnp.einsum(
        "nir,nji->njr", grad_first, first_up, preferred_element_type=jnp.float32
    ).reshape(cotangent.shape)
    terms = (grad_first_up, grad_second_up, grad_first_down, grad_second_down)
    if held is not None:
        return (grad_input, terms, held)
    return (grad_input, terms)


def body(arriving, stash, grad_in, first_up, second_up, first_down, second_down):
    activation = arriving[0]
    cotangent = grad_in[0]
    up_first = first_up[0]
    up_second = second_up[0]
    down_first = first_down[0]
    down_second = second_down[0]
    blocks = up_first.shape[0]
    width = up_first.shape[1]
    rows = activation.shape[1]
    current = activation.astype(jnp.bfloat16)
    folded_ahead = front(current.reshape(blocks, width, rows), up_first, up_second, down_first)[3]
    output = activation + jnp.einsum(
        "nir,nik->nkr", folded_ahead, down_second, preferred_element_type=jnp.float32
    ).reshape(activation.shape)
    sent = output.astype(jnp.bfloat16)
    near_activation = shifted(sent, "pipe", 1)
    sent, cotangent = lax.optimization_barrier((sent, cotangent))

    stored = stash[0, 0].reshape(blocks, width, rows)
    behind = front(stored, up_first, up_second, down_first)
    grad_step, totals = backward(
        stored, cotangent, up_first, up_second, down_first, down_second, behind
    )
    sent_back = (cotangent + grad_step).astype(jnp.bfloat16)
    near_cotangent = shifted(sent_back, "pipe", -1)
    near_activation, sent_back = lax.optimization_barrier((near_activation, sent_back))

    folded_ahead = front(near_activation.reshape(blocks, width, rows), up_first, up_second, down_first)[3]
    output = near_activation.astype(jnp.float32) + jnp.einsum(
        "nir,nik->nkr", folded_ahead, down_second, preferred_element_type=jnp.float32
    ).reshape(activation.shape)
    sent = output.astype(jnp.bfloat16)
    last_activation = shifted(sent, "pipe", 1)
    sent, near_cotangent = lax.optimization_barrier((sent, near_cotangent))

    stored = stash[1, 0].reshape(blocks, width, rows)
    behind = front(stored, up_first, up_second, down_first)
    grad_step, terms, last_activation = backward(
        stored, near_cotangent, up_first, up_second, down_first, down_second, behind,
        last_activation,
    )
    sent_back = (near_cotangent.astype(jnp.float32) + grad_step).astype(jnp.bfloat16)
    last_cotangent = shifted(sent_back, "pipe", -1)
    activation = last_activation.astype(jnp.float32)
    cotangent = last_cotangent.astype(jnp.float32)
    totals = (
        totals[0] + terms[0],
        totals[1] + terms[1],
        totals[2] + terms[2],
        totals[3] + terms[3],
    )
    return (
        activation[None],
        cotangent[None],
        totals[0][None],
        totals[1][None],
        totals[2][None],
        totals[3][None],
    )


def solution(mesh):
    placed = (
        P("pipe", "tensor", None),
        P(None, "pipe", "tensor", None),
        P("pipe", "tensor", None),
        P("pipe", "tensor", None, None),
        P("pipe", "tensor", None, None),
        P("pipe", "tensor", None, None),
        P("pipe", "tensor", None, None),
    )
    return jax.shard_map(
        body,
        mesh=mesh,
        in_specs=placed,
        out_specs=(
            P("pipe", "tensor", None),
            P("pipe", "tensor", None),
            P("pipe", "tensor", None, None),
            P("pipe", "tensor", None, None),
            P("pipe", "tensor", None, None),
            P("pipe", "tensor", None, None),
        ),
        check_vma=False,
    )
```

```python
import jax
import jax.numpy as jnp
from jax import lax
from jax.sharding import PartitionSpec as P


def shifted(value, axis, by):
    count = lax.axis_size(axis)
    return lax.ppermute(value, axis, [(i, (i + by) % count) for i in range(count)])


def smooth(values):
    return jax.nn.gelu(values, approximate=True)


def to_columns(value):
    return lax.all_to_all(value, "tensor", split_axis=1, concat_axis=0, tiled=True)


def to_rows(value):
    return lax.all_to_all(value, "tensor", split_axis=0, concat_axis=1, tiled=True)


def front(narrow_in, first_up, second_up, first_down):
    first_out = jnp.einsum(
        "njr,nji->nir", narrow_in, first_up, preferred_element_type=jnp.float32
    ).astype(jnp.bfloat16)
    spread = to_columns(first_out)
    hidden_pre = jnp.einsum("nir,inf->ifr", spread, second_up, preferred_element_type=jnp.float32)
    hidden = smooth(hidden_pre).astype(jnp.bfloat16)
    local_fold = jnp.einsum(
        "ifr,inf->nir", hidden, first_down, preferred_element_type=jnp.float32
    ).astype(jnp.bfloat16)
    folded = to_rows(local_fold)
    return (spread, hidden_pre, hidden, folded)


def backward(narrow_in, cotangent, first_up, second_up, first_down, second_down, parts, held=None):
    spread, hidden_pre, hidden, folded = parts
    narrow_grad = cotangent.astype(jnp.bfloat16).reshape(narrow_in.shape)
    grad_second_down = jnp.einsum(
        "nir,nkr->nik", folded, narrow_grad, preferred_element_type=jnp.float32
    )
    local_grad = jnp.einsum(
        "nkr,nik->nir", narrow_grad, second_down, preferred_element_type=jnp.float32
    ).astype(jnp.bfloat16)
    grad_folded = to_columns(local_grad)
    grad_first_down = jnp.einsum(
        "ifr,nir->inf", hidden, grad_folded, preferred_element_type=jnp.float32
    )
    grad_hidden = jnp.einsum(
        "nir,inf->ifr", grad_folded, first_down, preferred_element_type=jnp.float32
    )
    smooth_back = jax.vjp(smooth, hidden_pre)[1]
    grad_pre = smooth_back(grad_hidden)[0].astype(jnp.bfloat16)
    grad_second_up = jnp.einsum(
        "nir,ifr->inf", spread, grad_pre, preferred_element_type=jnp.float32
    )
    column_grad = jnp.einsum(
        "ifr,inf->nir", grad_pre, second_up, preferred_element_type=jnp.float32
    ).astype(jnp.bfloat16)
    if held is not None:
        column_grad, held = lax.optimization_barrier((column_grad, held))
    grad_first = to_rows(column_grad)
    grad_first_up = jnp.einsum(
        "njr,nir->nji", narrow_in, grad_first, preferred_element_type=jnp.float32
    )
    grad_input = jnp.einsum(
        "nir,nji->njr", grad_first, first_up, preferred_element_type=jnp.float32
    ).reshape(cotangent.shape)
    terms = (grad_first_up, grad_second_up, grad_first_down, grad_second_down)
    if held is not None:
        return (grad_input, terms, held)
    return (grad_input, terms)


def body(arriving, stash, grad_in, first_up, second_up, first_down, second_down):
    activation = arriving[0]
    cotangent = grad_in[0]
    up_first = first_up[0]
    up_second = second_up[0]
    down_first = first_down[0]
    down_second = second_down[0]
    blocks = up_first.shape[0]
    width = up_first.shape[1]
    rows = activation.shape[1]
    current = activation.astype(jnp.bfloat16)
    folded_ahead = front(current.reshape(blocks, width, rows), up_first, up_second, down_first)[3]
    output = activation + jnp.einsum(
        "nir,nik->nkr", folded_ahead, down_second, preferred_element_type=jnp.float32
    ).reshape(activation.shape)
    sent = output.astype(jnp.bfloat16)
    near_activation = shifted(sent, "pipe", 1)
    sent, cotangent = lax.optimization_barrier((sent, cotangent))

    replays = front(
        stash[:, 0].transpose(1, 0, 2).reshape(blocks, width, 2 * rows),
        up_first, up_second, down_first,
    )
    behind = tuple(value[..., :rows] for value in replays)
    stored = stash[0, 0].reshape(blocks, width, rows)
    grad_step, totals = backward(
        stored, cotangent, up_first, up_second, down_first, down_second, behind
    )
    sent_back = (cotangent + grad_step).astype(jnp.bfloat16)
    near_cotangent = shifted(sent_back, "pipe", -1)
    near_activation, sent_back = lax.optimization_barrier((near_activation, sent_back))

    folded_ahead = front(near_activation.reshape(blocks, width, rows), up_first, up_second, down_first)[3]
    output = near_activation.astype(jnp.float32) + jnp.einsum(
        "nir,nik->nkr", folded_ahead, down_second, preferred_element_type=jnp.float32
    ).reshape(activation.shape)
    sent = output.astype(jnp.bfloat16)
    last_activation = shifted(sent, "pipe", 1)
    sent, near_cotangent = lax.optimization_barrier((sent, near_cotangent))

    stored = stash[1, 0].reshape(blocks, width, rows)
    behind = tuple(value[..., rows:] for value in replays)
    grad_step, terms, last_activation = backward(
        stored, near_cotangent, up_first, up_second, down_first, down_second, behind,
        last_activation,
    )
    sent_back = (near_cotangent.astype(jnp.float32) + grad_step).astype(jnp.bfloat16)
    last_cotangent = shifted(sent_back, "pipe", -1)
    activation = last_activation.astype(jnp.float32)
    cotangent = last_cotangent.astype(jnp.float32)
    totals = (
        totals[0] + terms[0],
        totals[1] + terms[1],
        totals[2] + terms[2],
        totals[3] + terms[3],
    )
    return (
        activation[None],
        cotangent[None],
        totals[0][None],
        totals[1][None],
        totals[2][None],
        totals[3][None],
    )


def solution(mesh):
    placed = (
        P("pipe", "tensor", None),
        P(None, "pipe", "tensor", None),
        P("pipe", "tensor", None),
        P("pipe", "tensor", None, None),
        P("pipe", "tensor", None, None),
        P("pipe", "tensor", None, None),
        P("pipe", "tensor", None, None),
    )
    return jax.shard_map(
        body,
        mesh=mesh,
        in_specs=placed,
        out_specs=(
            P("pipe", "tensor", None),
            P("pipe", "tensor", None),
            P("pipe", "tensor", None, None),
            P("pipe", "tensor", None, None),
            P("pipe", "tensor", None, None),
            P("pipe", "tensor", None, None),
        ),
        check_vma=False,
    )
```

```python
import jax
import jax.numpy as jnp
from jax import lax
from jax.sharding import PartitionSpec as P


def shifted(value, axis, by):
    count = lax.axis_size(axis)
    return lax.ppermute(value, axis, [(i, (i + by) % count) for i in range(count)])


def smooth(values):
    return jax.nn.gelu(values, approximate=True)


def to_columns(value):
    return lax.all_to_all(value, "tensor", split_axis=1, concat_axis=0, tiled=True)


def to_rows(value):
    return lax.all_to_all(value, "tensor", split_axis=0, concat_axis=1, tiled=True)


def front(narrow_in, first_up, second_up, first_down):
    first_out = jnp.einsum(
        "njr,nji->nir", narrow_in, first_up, preferred_element_type=jnp.float32
    ).astype(jnp.bfloat16)
    spread = to_columns(first_out)
    hidden_pre = jnp.einsum("nir,inf->ifr", spread, second_up, preferred_element_type=jnp.float32)
    hidden = smooth(hidden_pre).astype(jnp.bfloat16)
    local_fold = jnp.einsum(
        "ifr,inf->nir", hidden, first_down, preferred_element_type=jnp.float32
    ).astype(jnp.bfloat16)
    folded = to_rows(local_fold)
    return (spread, hidden_pre, hidden, folded)


def backward(narrow_in, cotangent, first_up, second_up, first_down, second_down, parts, held=None):
    spread, hidden_pre, hidden, folded = parts
    narrow_grad = cotangent.astype(jnp.bfloat16).reshape(narrow_in.shape)
    grad_second_down = jnp.einsum(
        "nir,nkr->nik", folded, narrow_grad, preferred_element_type=jnp.float32
    )
    local_grad = jnp.einsum(
        "nkr,nik->nir", narrow_grad, second_down, preferred_element_type=jnp.float32
    ).astype(jnp.bfloat16)
    grad_folded = to_columns(local_grad)
    grad_first_down = jnp.einsum(
        "ifr,nir->inf", hidden, grad_folded, preferred_element_type=jnp.float32
    )
    grad_hidden = jnp.einsum(
        "nir,inf->ifr", grad_folded, first_down, preferred_element_type=jnp.float32
    )
    smooth_back = jax.vjp(smooth, hidden_pre)[1]
    grad_pre = smooth_back(grad_hidden)[0].astype(jnp.bfloat16)
    grad_second_up = jnp.einsum(
        "nir,ifr->inf", spread, grad_pre, preferred_element_type=jnp.float32
    )
    column_grad = jnp.einsum(
        "ifr,inf->nir", grad_pre, second_up, preferred_element_type=jnp.float32
    ).astype(jnp.bfloat16)
    if held is not None:
        column_grad, held = lax.optimization_barrier((column_grad, held))
    grad_first = to_rows(column_grad)
    grad_first_up = jnp.einsum(
        "njr,nir->nji", narrow_in, grad_first, preferred_element_type=jnp.float32
    )
    grad_input = jnp.einsum(
        "nir,nji->njr", grad_first, first_up, preferred_element_type=jnp.float32
    ).reshape(cotangent.shape)
    terms = (grad_first_up, grad_second_up, grad_first_down, grad_second_down)
    if held is not None:
        return (grad_input, terms, held)
    return (grad_input, terms)


def body(arriving, stash, grad_in, first_up, second_up, first_down, second_down):
    activation = arriving[0]
    cotangent = grad_in[0]
    up_first = first_up[0]
    up_second = second_up[0]
    down_first = first_down[0]
    down_second = second_down[0]
    blocks = up_first.shape[0]
    width = up_first.shape[1]
    rows = activation.shape[1]
    current = activation.astype(jnp.bfloat16)
    folded_ahead = front(current.reshape(blocks, width, rows), up_first, up_second, down_first)[3]
    output = activation + jnp.einsum(
        "nir,nik->nkr", folded_ahead, down_second, preferred_element_type=jnp.float32
    ).reshape(activation.shape)
    sent = output.astype(jnp.bfloat16)
    near_activation = shifted(sent, "pipe", 1)

    stored = stash[0, 0].reshape(blocks, width, rows)
    behind = front(stored, up_first, up_second, down_first)
    grad_step, totals = backward(
        stored, cotangent, up_first, up_second, down_first, down_second, behind
    )
    sent_back = (cotangent + grad_step).astype(jnp.bfloat16)
    near_cotangent = shifted(sent_back, "pipe", -1)
    near_activation, sent_back = lax.optimization_barrier((near_activation, sent_back))

    folded_ahead = front(near_activation.reshape(blocks, width, rows), up_first, up_second, down_first)[3]
    output = near_activation.astype(jnp.float32) + jnp.einsum(
        "nir,nik->nkr", folded_ahead, down_second, preferred_element_type=jnp.float32
    ).reshape(activation.shape)
    sent = output.astype(jnp.bfloat16)
    last_activation = shifted(sent, "pipe", 1)

    stored = stash[1, 0].reshape(blocks, width, rows)
    behind = front(stored, up_first, up_second, down_first)
    grad_step, terms, last_activation = backward(
        stored, near_cotangent, up_first, up_second, down_first, down_second, behind,
        last_activation,
    )
    sent_back = (near_cotangent.astype(jnp.float32) + grad_step).astype(jnp.bfloat16)
    last_cotangent = shifted(sent_back, "pipe", -1)
    activation = last_activation.astype(jnp.float32)
    cotangent = last_cotangent.astype(jnp.float32)
    totals = (
        totals[0] + terms[0],
        totals[1] + terms[1],
        totals[2] + terms[2],
        totals[3] + terms[3],
    )
    return (
        activation[None],
        cotangent[None],
        totals[0][None],
        totals[1][None],
        totals[2][None],
        totals[3][None],
    )


def solution(mesh):
    placed = (
        P("pipe", "tensor", None),
        P(None, "pipe", "tensor", None),
        P("pipe", "tensor", None),
        P("pipe", "tensor", None, None),
        P("pipe", "tensor", None, None),
        P("pipe", "tensor", None, None),
        P("pipe", "tensor", None, None),
    )
    return jax.shard_map(
        body,
        mesh=mesh,
        in_specs=placed,
        out_specs=(
            P("pipe", "tensor", None),
            P("pipe", "tensor", None),
            P("pipe", "tensor", None, None),
            P("pipe", "tensor", None, None),
            P("pipe", "tensor", None, None),
            P("pipe", "tensor", None, None),
        ),
        check_vma=False,
    )
```

```python
import jax
import jax.numpy as jnp
from jax import lax
from jax.sharding import PartitionSpec as P


def shifted(value, axis, by):
    count = lax.axis_size(axis)
    return lax.ppermute(value, axis, [(i, (i + by) % count) for i in range(count)])


def smooth(values):
    return jax.nn.gelu(values, approximate=True)


def to_columns(value):
    return lax.all_to_all(value, "tensor", split_axis=1, concat_axis=0, tiled=True)


def to_rows(value):
    return lax.all_to_all(value, "tensor", split_axis=0, concat_axis=1, tiled=True)


def front(narrow_in, first_up, second_up, first_down):
    first_out = jnp.einsum(
        "njr,nji->nir", narrow_in, first_up, preferred_element_type=jnp.float32
    ).astype(jnp.bfloat16)
    spread = to_columns(first_out)
    hidden_pre = jnp.einsum("nir,inf->ifr", spread, second_up, preferred_element_type=jnp.float32)
    hidden = smooth(hidden_pre).astype(jnp.bfloat16)
    local_fold = jnp.einsum(
        "ifr,inf->nir", hidden, first_down, preferred_element_type=jnp.float32
    ).astype(jnp.bfloat16)
    folded = to_rows(local_fold)
    return (spread, hidden_pre, hidden, folded)


def backward(narrow_in, cotangent, first_up, second_up, first_down, second_down, parts, held=None):
    spread, hidden_pre, hidden, folded = parts
    narrow_grad = cotangent.astype(jnp.bfloat16).reshape(narrow_in.shape)
    grad_second_down = jnp.einsum(
        "nir,nkr->nik", folded, narrow_grad, preferred_element_type=jnp.float32
    )
    local_grad = jnp.einsum(
        "nkr,nik->nir", narrow_grad, second_down, preferred_element_type=jnp.float32
    ).astype(jnp.bfloat16)
    grad_folded = to_columns(local_grad)
    grad_first_down = jnp.einsum(
        "ifr,nir->inf", hidden, grad_folded, preferred_element_type=jnp.float32
    )
    grad_hidden = jnp.einsum(
        "nir,inf->ifr", grad_folded, first_down, preferred_element_type=jnp.float32
    )
    smooth_back = jax.vjp(smooth, hidden_pre)[1]
    grad_pre = smooth_back(grad_hidden)[0].astype(jnp.bfloat16)
    grad_second_up = jnp.einsum(
        "nir,ifr->inf", spread, grad_pre, preferred_element_type=jnp.float32
    )
    column_grad = jnp.einsum(
        "ifr,inf->nir", grad_pre, second_up, preferred_element_type=jnp.float32
    ).astype(jnp.bfloat16)
    if held is not None:
        column_grad, held = lax.optimization_barrier((column_grad, held))
    grad_first = to_rows(column_grad)
    grad_first_up = jnp.einsum(
        "njr,nir->nji", narrow_in, grad_first, preferred_element_type=jnp.float32
    )
    grad_input = jnp.einsum(
        "nir,nji->njr", grad_first, first_up, preferred_element_type=jnp.float32
    ).reshape(cotangent.shape)
    terms = (grad_first_up, grad_second_up, grad_first_down, grad_second_down)
    if held is not None:
        return (grad_input, terms, held)
    return (grad_input, terms)


def body(arriving, stash, grad_in, first_up, second_up, first_down, second_down):
    activation = arriving[0]
    cotangent = grad_in[0]
    up_first = first_up[0]
    up_second = second_up[0]
    down_first = first_down[0]
    down_second = second_down[0]
    blocks = up_first.shape[0]
    width = up_first.shape[1]
    rows = activation.shape[1]
    current = activation.astype(jnp.bfloat16)
    folded_ahead = front(current.reshape(blocks, width, rows), up_first, up_second, down_first)[3]
    output = activation + jnp.einsum(
        "nir,nik->nkr", folded_ahead, down_second, preferred_element_type=jnp.float32
    ).reshape(activation.shape)
    sent = output.astype(jnp.bfloat16)
    near_activation = shifted(sent, "pipe", 1)

    stored = stash[0, 0].reshape(blocks, width, rows)
    behind = front(stored, up_first, up_second, down_first)
    grad_step, totals = backward(
        stored, cotangent, up_first, up_second, down_first, down_second, behind
    )
    sent_back = (cotangent + grad_step).astype(jnp.bfloat16)
    later, sent_back = lax.optimization_barrier((stash[1, 0], sent_back))
    near_cotangent = shifted(sent_back, "pipe", -1)
    near_activation, sent_back = lax.optimization_barrier((near_activation, sent_back))

    folded_ahead = front(near_activation.reshape(blocks, width, rows), up_first, up_second, down_first)[3]
    output = near_activation.astype(jnp.float32) + jnp.einsum(
        "nir,nik->nkr", folded_ahead, down_second, preferred_element_type=jnp.float32
    ).reshape(activation.shape)
    sent = output.astype(jnp.bfloat16)
    last_activation = shifted(sent, "pipe", 1)

    stored = later.reshape(blocks, width, rows)
    behind = front(stored, up_first, up_second, down_first)
    grad_step, terms, last_activation = backward(
        stored, near_cotangent, up_first, up_second, down_first, down_second, behind,
        last_activation,
    )
    sent_back = (near_cotangent.astype(jnp.float32) + grad_step).astype(jnp.bfloat16)
    last_cotangent = shifted(sent_back, "pipe", -1)
    activation = last_activation.astype(jnp.float32)
    cotangent = last_cotangent.astype(jnp.float32)
    totals = (
        totals[0] + terms[0],
        totals[1] + terms[1],
        totals[2] + terms[2],
        totals[3] + terms[3],
    )
    return (
        activation[None],
        cotangent[None],
        totals[0][None],
        totals[1][None],
        totals[2][None],
        totals[3][None],
    )


def solution(mesh):
    placed = (
        P("pipe", "tensor", None),
        P(None, "pipe", "tensor", None),
        P("pipe", "tensor", None),
        P("pipe", "tensor", None, None),
        P("pipe", "tensor", None, None),
        P("pipe", "tensor", None, None),
        P("pipe", "tensor", None, None),
    )
    return jax.shard_map(
        body,
        mesh=mesh,
        in_specs=placed,
        out_specs=(
            P("pipe", "tensor", None),
            P("pipe", "tensor", None),
            P("pipe", "tensor", None, None),
            P("pipe", "tensor", None, None),
            P("pipe", "tensor", None, None),
            P("pipe", "tensor", None, None),
        ),
        check_vma=False,
    )
```

```python
import jax
import jax.numpy as jnp
from jax import lax
from jax.sharding import PartitionSpec as P


def shifted(value, axis, by):
    count = lax.axis_size(axis)
    return lax.ppermute(value, axis, [(i, (i + by) % count) for i in range(count)])


def smooth(values):
    return jax.nn.gelu(values, approximate=True)


def to_columns(value):
    return lax.all_to_all(value, "tensor", split_axis=1, concat_axis=0, tiled=True)


def to_rows(value):
    return lax.all_to_all(value, "tensor", split_axis=0, concat_axis=1, tiled=True)


def front(narrow_in, first_up, second_up, first_down):
    first_out = jnp.einsum(
        "njr,nji->nir", narrow_in, first_up, preferred_element_type=jnp.float32
    ).astype(jnp.bfloat16)
    spread = to_columns(first_out)
    hidden_pre = jnp.einsum("nir,inf->ifr", spread, second_up, preferred_element_type=jnp.float32)
    hidden = smooth(hidden_pre).astype(jnp.bfloat16)
    local_fold = jnp.einsum(
        "ifr,inf->nir", hidden, first_down, preferred_element_type=jnp.float32
    ).astype(jnp.bfloat16)
    folded = to_rows(local_fold)
    return (spread, hidden_pre, hidden, folded)


def backward(narrow_in, cotangent, first_up, second_up, first_down, second_down, parts, held=None):
    spread, hidden_pre, hidden, folded = parts
    narrow_grad = cotangent.astype(jnp.bfloat16).reshape(narrow_in.shape)
    grad_second_down = jnp.einsum(
        "nir,nkr->nik", folded, narrow_grad, preferred_element_type=jnp.float32
    )
    local_grad = jnp.einsum(
        "nkr,nik->nir", narrow_grad, second_down, preferred_element_type=jnp.float32
    ).astype(jnp.bfloat16)
    grad_folded = to_columns(local_grad)
    grad_first_down = jnp.einsum(
        "ifr,nir->inf", hidden, grad_folded, preferred_element_type=jnp.float32
    )
    grad_hidden = jnp.einsum(
        "nir,inf->ifr", grad_folded, first_down, preferred_element_type=jnp.float32
    )
    smooth_back = jax.vjp(smooth, hidden_pre)[1]
    grad_pre = smooth_back(grad_hidden)[0].astype(jnp.bfloat16)
    grad_second_up = jnp.einsum(
        "nir,ifr->inf", spread, grad_pre, preferred_element_type=jnp.float32
    )
    column_grad = jnp.einsum(
        "ifr,inf->nir", grad_pre, second_up, preferred_element_type=jnp.float32
    ).astype(jnp.bfloat16)
    if held is not None:
        column_grad, held = lax.optimization_barrier((column_grad, held))
    grad_first = to_rows(column_grad)
    grad_first_up = jnp.einsum(
        "njr,nir->nji", narrow_in, grad_first, preferred_element_type=jnp.float32
    )
    grad_input = jnp.einsum(
        "nir,nji->njr", grad_first, first_up, preferred_element_type=jnp.float32
    ).reshape(cotangent.shape)
    terms = (grad_first_up, grad_second_up, grad_first_down, grad_second_down)
    if held is not None:
        return (grad_input, terms, held)
    return (grad_input, terms)


def body(arriving, stash, grad_in, first_up, second_up, first_down, second_down):
    activation = arriving[0]
    cotangent = grad_in[0]
    up_first = first_up[0]
    up_second = second_up[0]
    down_first = first_down[0]
    down_second = second_down[0]
    blocks = up_first.shape[0]
    width = up_first.shape[1]
    rows = activation.shape[1]
    current = activation.astype(jnp.bfloat16)
    folded_ahead = front(current.reshape(blocks, width, rows), up_first, up_second, down_first)[3]
    output = activation + jnp.einsum(
        "nir,nik->nkr", folded_ahead, down_second, preferred_element_type=jnp.float32
    ).reshape(activation.shape)
    sent = output.astype(jnp.bfloat16)
    near_activation = shifted(sent, "pipe", 1)

    stored = stash[0, 0].reshape(blocks, width, rows)
    behind = front(stored, up_first, up_second, down_first)
    grad_step, totals = backward(
        stored, cotangent, up_first, up_second, down_first, down_second, behind
    )
    sent_back = (cotangent + grad_step).astype(jnp.bfloat16)
    near_activation, sent_back = lax.optimization_barrier((near_activation, sent_back))
    near_cotangent = shifted(sent_back, "pipe", -1)

    folded_ahead = front(near_activation.reshape(blocks, width, rows), up_first, up_second, down_first)[3]
    output = near_activation.astype(jnp.float32) + jnp.einsum(
        "nir,nik->nkr", folded_ahead, down_second, preferred_element_type=jnp.float32
    ).reshape(activation.shape)
    sent = output.astype(jnp.bfloat16)
    last_activation = shifted(sent, "pipe", 1)

    stored = stash[1, 0].reshape(blocks, width, rows)
    behind = front(stored, up_first, up_second, down_first)
    grad_step, terms, last_activation = backward(
        stored, near_cotangent, up_first, up_second, down_first, down_second, behind,
        last_activation,
    )
    sent_back = (near_cotangent.astype(jnp.float32) + grad_step).astype(jnp.bfloat16)
    last_cotangent = shifted(sent_back, "pipe", -1)
    activation = last_activation.astype(jnp.float32)
    cotangent = last_cotangent.astype(jnp.float32)
    totals = (
        totals[0] + terms[0],
        totals[1] + terms[1],
        totals[2] + terms[2],
        totals[3] + terms[3],
    )
    return (
        activation[None],
        cotangent[None],
        totals[0][None],
        totals[1][None],
        totals[2][None],
        totals[3][None],
    )


def solution(mesh):
    placed = (
        P("pipe", "tensor", None),
        P(None, "pipe", "tensor", None),
        P("pipe", "tensor", None),
        P("pipe", "tensor", None, None),
        P("pipe", "tensor", None, None),
        P("pipe", "tensor", None, None),
        P("pipe", "tensor", None, None),
    )
    return jax.shard_map(
        body,
        mesh=mesh,
        in_specs=placed,
        out_specs=(
            P("pipe", "tensor", None),
            P("pipe", "tensor", None),
            P("pipe", "tensor", None, None),
            P("pipe", "tensor", None, None),
            P("pipe", "tensor", None, None),
            P("pipe", "tensor", None, None),
        ),
        check_vma=False,
    )
```

```python
import jax
import jax.numpy as jnp
from jax import lax
from jax.sharding import PartitionSpec as P


def shifted(value, axis, by):
    count = lax.axis_size(axis)
    return lax.ppermute(value, axis, [(i, (i + by) % count) for i in range(count)])


def smooth(values):
    return jax.nn.gelu(values, approximate=True)


def to_columns(value):
    return lax.all_to_all(value, "tensor", split_axis=1, concat_axis=0, tiled=True)


def to_rows(value):
    return lax.all_to_all(value, "tensor", split_axis=0, concat_axis=1, tiled=True)


def front(narrow_in, first_up, second_up, first_down):
    first_out = jnp.einsum(
        "njr,nji->nir", narrow_in, first_up, preferred_element_type=jnp.float32
    ).astype(jnp.bfloat16)
    spread = to_columns(first_out)
    hidden_pre = jnp.einsum("nir,inf->ifr", spread, second_up, preferred_element_type=jnp.float32)
    hidden = smooth(hidden_pre).astype(jnp.bfloat16)
    local_fold = jnp.einsum(
        "ifr,inf->nir", hidden, first_down, preferred_element_type=jnp.float32
    ).astype(jnp.bfloat16)
    folded = to_rows(local_fold)
    return (spread, hidden_pre, hidden, folded)


def backward(narrow_in, cotangent, first_up, second_up, first_down, second_down, parts, held=None):
    spread, hidden_pre, hidden, folded = parts
    narrow_grad = cotangent.astype(jnp.bfloat16).reshape(narrow_in.shape)
    grad_second_down = jnp.einsum(
        "nir,nkr->nik", folded, narrow_grad, preferred_element_type=jnp.float32
    )
    local_grad = jnp.einsum(
        "nkr,nik->nir", narrow_grad, second_down, preferred_element_type=jnp.float32
    ).astype(jnp.bfloat16)
    grad_folded = to_columns(local_grad)
    grad_first_down = jnp.einsum(
        "ifr,nir->inf", hidden, grad_folded, preferred_element_type=jnp.float32
    )
    grad_hidden = jnp.einsum(
        "nir,inf->ifr", grad_folded, first_down, preferred_element_type=jnp.float32
    )
    smooth_back = jax.vjp(smooth, hidden_pre)[1]
    grad_pre = smooth_back(grad_hidden)[0].astype(jnp.bfloat16)
    grad_second_up = jnp.einsum(
        "nir,ifr->inf", spread, grad_pre, preferred_element_type=jnp.float32
    )
    column_grad = jnp.einsum(
        "ifr,inf->nir", grad_pre, second_up, preferred_element_type=jnp.float32
    ).astype(jnp.bfloat16)
    if held is not None:
        column_grad, held = lax.optimization_barrier((column_grad, held))
    grad_first = to_rows(column_grad)
    grad_first_up = jnp.einsum(
        "njr,nir->nji", narrow_in, grad_first, preferred_element_type=jnp.float32
    )
    grad_input = jnp.einsum(
        "nir,nji->njr", grad_first, first_up, preferred_element_type=jnp.float32
    ).reshape(cotangent.shape)
    terms = (grad_first_up, grad_second_up, grad_first_down, grad_second_down)
    if held is not None:
        return (grad_input, terms, held)
    return (grad_input, terms)


def body(arriving, stash, grad_in, first_up, second_up, first_down, second_down):
    activation = arriving[0]
    cotangent = grad_in[0]
    up_first = first_up[0]
    up_second = second_up[0]
    down_first = first_down[0]
    down_second = second_down[0]
    blocks = up_first.shape[0]
    width = up_first.shape[1]
    rows = activation.shape[1]
    current = activation.astype(jnp.bfloat16)
    ahead = front(current.reshape(blocks, width, rows), up_first, up_second, down_first)
    folded_ahead = ahead[3]
    first_stored, _ = lax.optimization_barrier((stash[0, 0], ahead[0]))
    cotangent, later, _ = lax.optimization_barrier((cotangent, stash[1, 0], folded_ahead))
    output = activation + jnp.einsum(
        "nir,nik->nkr", folded_ahead, down_second, preferred_element_type=jnp.float32
    ).reshape(activation.shape)
    sent = output.astype(jnp.bfloat16)
    near_activation = shifted(sent, "pipe", 1)

    stored = first_stored.reshape(blocks, width, rows)
    behind = front(stored, up_first, up_second, down_first)
    grad_step, totals = backward(
        stored, cotangent, up_first, up_second, down_first, down_second, behind
    )
    sent_back = (cotangent + grad_step).astype(jnp.bfloat16)
    near_activation, sent_back = lax.optimization_barrier((near_activation, sent_back))
    near_cotangent = shifted(sent_back, "pipe", -1)

    folded_ahead = front(near_activation.reshape(blocks, width, rows), up_first, up_second, down_first)[3]
    output = near_activation.astype(jnp.float32) + jnp.einsum(
        "nir,nik->nkr", folded_ahead, down_second, preferred_element_type=jnp.float32
    ).reshape(activation.shape)
    sent = output.astype(jnp.bfloat16)
    last_activation = shifted(sent, "pipe", 1)

    stored = later.reshape(blocks, width, rows)
    behind = front(stored, up_first, up_second, down_first)
    grad_step, terms, last_activation = backward(
        stored, near_cotangent, up_first, up_second, down_first, down_second, behind,
        last_activation,
    )
    sent_back = (near_cotangent.astype(jnp.float32) + grad_step).astype(jnp.bfloat16)
    last_cotangent = shifted(sent_back, "pipe", -1)
    activation = last_activation.astype(jnp.float32)
    cotangent = last_cotangent.astype(jnp.float32)
    totals = (
        totals[0] + terms[0],
        totals[1] + terms[1],
        totals[2] + terms[2],
        totals[3] + terms[3],
    )
    return (
        activation[None],
        cotangent[None],
        totals[0][None],
        totals[1][None],
        totals[2][None],
        totals[3][None],
    )


def solution(mesh):
    placed = (
        P("pipe", "tensor", None),
        P(None, "pipe", "tensor", None),
        P("pipe", "tensor", None),
        P("pipe", "tensor", None, None),
        P("pipe", "tensor", None, None),
        P("pipe", "tensor", None, None),
        P("pipe", "tensor", None, None),
    )
    return jax.shard_map(
        body,
        mesh=mesh,
        in_specs=placed,
        out_specs=(
            P("pipe", "tensor", None),
            P("pipe", "tensor", None),
            P("pipe", "tensor", None, None),
            P("pipe", "tensor", None, None),
            P("pipe", "tensor", None, None),
            P("pipe", "tensor", None, None),
        ),
        check_vma=False,
    )
```

```python
import jax
import jax.numpy as jnp
from jax import lax
from jax.sharding import PartitionSpec as P


def shifted(value, axis, by):
    count = lax.axis_size(axis)
    return lax.ppermute(value, axis, [(i, (i + by) % count) for i in range(count)])


def smooth(values):
    return jax.nn.gelu(values, approximate=True)


def to_columns(value):
    return lax.all_to_all(value, "tensor", split_axis=1, concat_axis=0, tiled=True)


def to_rows(value):
    return lax.all_to_all(value, "tensor", split_axis=0, concat_axis=1, tiled=True)


def front(narrow_in, first_up, second_up, first_down):
    first_out = jnp.einsum(
        "njr,nji->nir", narrow_in, first_up, preferred_element_type=jnp.float32
    ).astype(jnp.bfloat16)
    spread = to_columns(first_out)
    hidden_pre = jnp.einsum("nir,inf->ifr", spread, second_up, preferred_element_type=jnp.float32)
    hidden = smooth(hidden_pre).astype(jnp.bfloat16)
    local_fold = jnp.einsum(
        "ifr,inf->nir", hidden, first_down, preferred_element_type=jnp.float32
    ).astype(jnp.bfloat16)
    folded = to_rows(local_fold)
    return (spread, hidden_pre, hidden, folded)


def backward(narrow_in, cotangent, first_up, second_up, first_down, second_down, parts, held=None):
    spread, hidden_pre, hidden, folded = parts
    narrow_grad = cotangent.astype(jnp.bfloat16).reshape(narrow_in.shape)
    grad_second_down = jnp.einsum(
        "nir,nkr->nik", folded, narrow_grad, preferred_element_type=jnp.float32
    )
    local_grad = jnp.einsum(
        "nkr,nik->nir", narrow_grad, second_down, preferred_element_type=jnp.float32
    ).astype(jnp.bfloat16)
    grad_folded = to_columns(local_grad)
    grad_first_down = jnp.einsum(
        "ifr,nir->inf", hidden, grad_folded, preferred_element_type=jnp.float32
    )
    grad_hidden = jnp.einsum(
        "nir,inf->ifr", grad_folded, first_down, preferred_element_type=jnp.float32
    )
    smooth_back = jax.vjp(smooth, hidden_pre)[1]
    grad_pre = smooth_back(grad_hidden)[0].astype(jnp.bfloat16)
    grad_second_up = jnp.einsum(
        "nir,ifr->inf", spread, grad_pre, preferred_element_type=jnp.float32
    )
    column_grad = jnp.einsum(
        "ifr,inf->nir", grad_pre, second_up, preferred_element_type=jnp.float32
    ).astype(jnp.bfloat16)
    grad_first = to_rows(column_grad)
    if held is not None:
        grad_first, held = lax.optimization_barrier((grad_first, held))
    grad_first_up = jnp.einsum(
        "njr,nir->nji", narrow_in, grad_first, preferred_element_type=jnp.float32
    )
    grad_input = jnp.einsum(
        "nir,nji->njr", grad_first, first_up, preferred_element_type=jnp.float32
    ).reshape(cotangent.shape)
    terms = (grad_first_up, grad_second_up, grad_first_down, grad_second_down)
    if held is not None:
        return (grad_input, terms, held)
    return (grad_input, terms)


def body(arriving, stash, grad_in, first_up, second_up, first_down, second_down):
    activation = arriving[0]
    cotangent = grad_in[0]
    up_first = first_up[0]
    up_second = second_up[0]
    down_first = first_down[0]
    down_second = second_down[0]
    blocks = up_first.shape[0]
    width = up_first.shape[1]
    rows = activation.shape[1]
    current = activation.astype(jnp.bfloat16)
    folded_ahead = front(current.reshape(blocks, width, rows), up_first, up_second, down_first)[3]
    output = activation + jnp.einsum(
        "nir,nik->nkr", folded_ahead, down_second, preferred_element_type=jnp.float32
    ).reshape(activation.shape)
    sent = output.astype(jnp.bfloat16)
    near_activation = shifted(sent, "pipe", 1)

    stored = stash[0, 0].reshape(blocks, width, rows)
    behind = front(stored, up_first, up_second, down_first)
    grad_step, totals = backward(
        stored, cotangent, up_first, up_second, down_first, down_second, behind
    )
    sent_back = (cotangent + grad_step).astype(jnp.bfloat16)
    near_activation, sent_back = lax.optimization_barrier((near_activation, sent_back))
    near_cotangent = shifted(sent_back, "pipe", -1)

    folded_ahead = front(near_activation.reshape(blocks, width, rows), up_first, up_second, down_first)[3]
    output = near_activation.astype(jnp.float32) + jnp.einsum(
        "nir,nik->nkr", folded_ahead, down_second, preferred_element_type=jnp.float32
    ).reshape(activation.shape)
    sent = output.astype(jnp.bfloat16)
    last_activation = shifted(sent, "pipe", 1)

    stored = stash[1, 0].reshape(blocks, width, rows)
    behind = front(stored, up_first, up_second, down_first)
    grad_step, terms, last_activation = backward(
        stored, near_cotangent, up_first, up_second, down_first, down_second, behind,
        last_activation,
    )
    sent_back = (near_cotangent.astype(jnp.float32) + grad_step).astype(jnp.bfloat16)
    last_cotangent = shifted(sent_back, "pipe", -1)
    activation = last_activation.astype(jnp.float32)
    cotangent = last_cotangent.astype(jnp.float32)
    totals = (
        totals[0] + terms[0],
        totals[1] + terms[1],
        totals[2] + terms[2],
        totals[3] + terms[3],
    )
    return (
        activation[None],
        cotangent[None],
        totals[0][None],
        totals[1][None],
        totals[2][None],
        totals[3][None],
    )


def solution(mesh):
    placed = (
        P("pipe", "tensor", None),
        P(None, "pipe", "tensor", None),
        P("pipe", "tensor", None),
        P("pipe", "tensor", None, None),
        P("pipe", "tensor", None, None),
        P("pipe", "tensor", None, None),
        P("pipe", "tensor", None, None),
    )
    return jax.shard_map(
        body,
        mesh=mesh,
        in_specs=placed,
        out_specs=(
            P("pipe", "tensor", None),
            P("pipe", "tensor", None),
            P("pipe", "tensor", None, None),
            P("pipe", "tensor", None, None),
            P("pipe", "tensor", None, None),
            P("pipe", "tensor", None, None),
        ),
        check_vma=False,
    )
```

```python
import jax
import jax.numpy as jnp
from jax import lax
from jax.sharding import PartitionSpec as P


def shifted(value, axis, by):
    count = lax.axis_size(axis)
    return lax.ppermute(value, axis, [(i, (i + by) % count) for i in range(count)])


def smooth(values):
    return jax.nn.gelu(values, approximate=True)


def to_columns(value):
    return lax.all_to_all(value, "tensor", split_axis=1, concat_axis=0, tiled=True)


def to_rows(value):
    return lax.all_to_all(value, "tensor", split_axis=0, concat_axis=1, tiled=True)


def front(narrow_in, first_up, second_up, first_down):
    first_out = jnp.einsum(
        "njr,nji->nir", narrow_in, first_up, preferred_element_type=jnp.float32
    ).astype(jnp.bfloat16)
    spread = to_columns(first_out)
    hidden_pre = jnp.einsum("nir,inf->ifr", spread, second_up, preferred_element_type=jnp.float32)
    hidden = smooth(hidden_pre).astype(jnp.bfloat16)
    local_fold = jnp.einsum(
        "ifr,inf->nir", hidden, first_down, preferred_element_type=jnp.float32
    ).astype(jnp.bfloat16)
    folded = to_rows(local_fold)
    return (spread, hidden_pre, hidden, folded)


def backward(narrow_in, cotangent, first_up, second_up, first_down, second_down, parts, held=None):
    spread, hidden_pre, hidden, folded = parts
    narrow_grad = cotangent.astype(jnp.bfloat16).reshape(narrow_in.shape)
    grad_second_down = jnp.einsum(
        "nir,nkr->nik", folded, narrow_grad, preferred_element_type=jnp.float32
    )
    local_grad = jnp.einsum(
        "nkr,nik->nir", narrow_grad, second_down, preferred_element_type=jnp.float32
    ).astype(jnp.bfloat16)
    grad_folded = to_columns(local_grad)
    grad_first_down = jnp.einsum(
        "ifr,nir->inf", hidden, grad_folded, preferred_element_type=jnp.float32
    )
    grad_hidden = jnp.einsum(
        "nir,inf->ifr", grad_folded, first_down, preferred_element_type=jnp.float32
    )
    smooth_back = jax.vjp(smooth, hidden_pre)[1]
    grad_pre = smooth_back(grad_hidden)[0].astype(jnp.bfloat16)
    grad_second_up = jnp.einsum(
        "nir,ifr->inf", spread, grad_pre, preferred_element_type=jnp.float32
    )
    column_grad = jnp.einsum(
        "ifr,inf->nir", grad_pre, second_up, preferred_element_type=jnp.float32
    ).astype(jnp.bfloat16)
    grad_first = to_rows(column_grad)
    if held is not None:
        grad_first, held = lax.optimization_barrier((grad_first, held))
    grad_first_up = jnp.einsum(
        "njr,nir->nji", narrow_in, grad_first, preferred_element_type=jnp.float32
    )
    grad_input = jnp.einsum(
        "nir,nji->njr", grad_first, first_up, preferred_element_type=jnp.float32
    ).reshape(cotangent.shape)
    terms = (grad_first_up, grad_second_up, grad_first_down, grad_second_down)
    if held is not None:
        return (grad_input, terms, held)
    return (grad_input, terms)


def body(arriving, stash, grad_in, first_up, second_up, first_down, second_down):
    activation = arriving[0]
    cotangent = grad_in[0]
    up_first = first_up[0]
    up_second = second_up[0]
    down_first = first_down[0]
    down_second = second_down[0]
    blocks = up_first.shape[0]
    width = up_first.shape[1]
    rows = activation.shape[1]
    current = activation.astype(jnp.bfloat16)
    folded_ahead = front(current.reshape(blocks, width, rows), up_first, up_second, down_first)[3]
    output = activation + jnp.einsum(
        "nir,nik->nkr", folded_ahead, down_second, preferred_element_type=jnp.float32
    ).reshape(activation.shape)
    sent = output.astype(jnp.bfloat16)
    near_activation = shifted(sent, "pipe", 1)

    stored = stash[0, 0].reshape(blocks, width, rows)
    behind = front(stored, up_first, up_second, down_first)
    grad_step, totals = backward(
        stored, cotangent, up_first, up_second, down_first, down_second, behind
    )
    sent_back = (cotangent + grad_step).astype(jnp.bfloat16)
    stored_later = stash[1, 0].reshape(blocks, width, rows)
    behind_later = front(stored_later, up_first, up_second, down_first)
    near_activation, sent_back, _ = lax.optimization_barrier(
        (near_activation, sent_back, behind_later[0])
    )
    near_cotangent = shifted(sent_back, "pipe", -1)

    folded_ahead = front(near_activation.reshape(blocks, width, rows), up_first, up_second, down_first)[3]
    output = near_activation.astype(jnp.float32) + jnp.einsum(
        "nir,nik->nkr", folded_ahead, down_second, preferred_element_type=jnp.float32
    ).reshape(activation.shape)
    sent = output.astype(jnp.bfloat16)
    last_activation = shifted(sent, "pipe", 1)

    stored = stored_later
    behind = behind_later
    grad_step, terms, last_activation = backward(
        stored, near_cotangent, up_first, up_second, down_first, down_second, behind,
        last_activation,
    )
    sent_back = (near_cotangent.astype(jnp.float32) + grad_step).astype(jnp.bfloat16)
    last_cotangent = shifted(sent_back, "pipe", -1)
    activation = last_activation.astype(jnp.float32)
    cotangent = last_cotangent.astype(jnp.float32)
    totals = (
        totals[0] + terms[0],
        totals[1] + terms[1],
        totals[2] + terms[2],
        totals[3] + terms[3],
    )
    return (
        activation[None],
        cotangent[None],
        totals[0][None],
        totals[1][None],
        totals[2][None],
        totals[3][None],
    )


def solution(mesh):
    placed = (
        P("pipe", "tensor", None),
        P(None, "pipe", "tensor", None),
        P("pipe", "tensor", None),
        P("pipe", "tensor", None, None),
        P("pipe", "tensor", None, None),
        P("pipe", "tensor", None, None),
        P("pipe", "tensor", None, None),
    )
    return jax.shard_map(
        body,
        mesh=mesh,
        in_specs=placed,
        out_specs=(
            P("pipe", "tensor", None),
            P("pipe", "tensor", None),
            P("pipe", "tensor", None, None),
            P("pipe", "tensor", None, None),
            P("pipe", "tensor", None, None),
            P("pipe", "tensor", None, None),
        ),
        check_vma=False,
    )
```

```python
import jax
import jax.numpy as jnp
from jax import lax
from jax.sharding import PartitionSpec as P


def shifted(value, axis, by):
    count = lax.axis_size(axis)
    return lax.ppermute(value, axis, [(i, (i + by) % count) for i in range(count)])


def smooth(values):
    return jax.nn.gelu(values, approximate=True)


def to_columns(value):
    return lax.all_to_all(value, "tensor", split_axis=1, concat_axis=0, tiled=True)


def to_rows(value):
    return lax.all_to_all(value, "tensor", split_axis=0, concat_axis=1, tiled=True)


def swapped(pieces):
    count = lax.axis_size("tensor")
    me = lax.axis_index("tensor")
    arrived = []
    for shift in range(count):
        piece = lax.dynamic_index_in_dim(pieces, (me + shift) % count, 0, keepdims=False)
        if shift:
            piece = lax.ppermute(
                piece, "tensor", [(i, (i + shift) % count) for i in range(count)]
            )
        arrived.append(piece)
    order = (me - jnp.arange(count)) % count
    return jnp.take(jnp.stack(arrived), order, axis=0)


def to_columns_by_permutes(value):
    count = lax.axis_size("tensor")
    pieces = value.reshape(value.shape[0], count, -1, value.shape[2]).swapaxes(0, 1)
    out = swapped(pieces)
    return out.reshape((-1,) + out.shape[2:])


def to_rows_by_permutes(value):
    count = lax.axis_size("tensor")
    out = swapped(value.reshape((count, -1) + value.shape[1:]))
    out = out.swapaxes(0, 1)
    return out.reshape(out.shape[0], -1, out.shape[3])


def front(narrow_in, first_up, second_up, first_down, columns=None, rows=None):
    columns = columns or to_columns
    rows = rows or to_rows
    first_out = jnp.einsum(
        "njr,nji->nir", narrow_in, first_up, preferred_element_type=jnp.float32
    ).astype(jnp.bfloat16)
    spread = columns(first_out)
    hidden_pre = jnp.einsum("nir,inf->ifr", spread, second_up, preferred_element_type=jnp.float32)
    hidden = smooth(hidden_pre).astype(jnp.bfloat16)
    local_fold = jnp.einsum(
        "ifr,inf->nir", hidden, first_down, preferred_element_type=jnp.float32
    ).astype(jnp.bfloat16)
    folded = rows(local_fold)
    return (spread, hidden_pre, hidden, folded)


def backward(narrow_in, cotangent, first_up, second_up, first_down, second_down, parts, held=None):
    spread, hidden_pre, hidden, folded = parts
    narrow_grad = cotangent.astype(jnp.bfloat16).reshape(narrow_in.shape)
    grad_second_down = jnp.einsum(
        "nir,nkr->nik", folded, narrow_grad, preferred_element_type=jnp.float32
    )
    local_grad = jnp.einsum(
        "nkr,nik->nir", narrow_grad, second_down, preferred_element_type=jnp.float32
    ).astype(jnp.bfloat16)
    grad_folded = to_columns(local_grad)
    grad_first_down = jnp.einsum(
        "ifr,nir->inf", hidden, grad_folded, preferred_element_type=jnp.float32
    )
    grad_hidden = jnp.einsum(
        "nir,inf->ifr", grad_folded, first_down, preferred_element_type=jnp.float32
    )
    smooth_back = jax.vjp(smooth, hidden_pre)[1]
    grad_pre = smooth_back(grad_hidden)[0].astype(jnp.bfloat16)
    grad_second_up = jnp.einsum(
        "nir,ifr->inf", spread, grad_pre, preferred_element_type=jnp.float32
    )
    column_grad = jnp.einsum(
        "ifr,inf->nir", grad_pre, second_up, preferred_element_type=jnp.float32
    ).astype(jnp.bfloat16)
    grad_first = to_rows(column_grad)
    if held is not None:
        grad_first, held = lax.optimization_barrier((grad_first, held))
    grad_first_up = jnp.einsum(
        "njr,nir->nji", narrow_in, grad_first, preferred_element_type=jnp.float32
    )
    grad_input = jnp.einsum(
        "nir,nji->njr", grad_first, first_up, preferred_element_type=jnp.float32
    ).reshape(cotangent.shape)
    terms = (grad_first_up, grad_second_up, grad_first_down, grad_second_down)
    if held is not None:
        return (grad_input, terms, held)
    return (grad_input, terms)


def body(arriving, stash, grad_in, first_up, second_up, first_down, second_down):
    activation = arriving[0]
    cotangent = grad_in[0]
    up_first = first_up[0]
    up_second = second_up[0]
    down_first = first_down[0]
    down_second = second_down[0]
    blocks = up_first.shape[0]
    width = up_first.shape[1]
    rows = activation.shape[1]
    current = activation.astype(jnp.bfloat16)
    folded_ahead = front(current.reshape(blocks, width, rows), up_first, up_second, down_first)[3]
    output = activation + jnp.einsum(
        "nir,nik->nkr", folded_ahead, down_second, preferred_element_type=jnp.float32
    ).reshape(activation.shape)
    sent = output.astype(jnp.bfloat16)
    near_activation = shifted(sent, "pipe", 1)

    stored = stash[0, 0].reshape(blocks, width, rows)
    behind = front(
        stored, up_first, up_second, down_first,
        to_columns_by_permutes, to_rows_by_permutes,
    )
    grad_step, totals = backward(
        stored, cotangent, up_first, up_second, down_first, down_second, behind
    )
    sent_back = (cotangent + grad_step).astype(jnp.bfloat16)
    near_activation, sent_back = lax.optimization_barrier((near_activation, sent_back))
    near_cotangent = shifted(sent_back, "pipe", -1)

    folded_ahead = front(near_activation.reshape(blocks, width, rows), up_first, up_second, down_first)[3]
    output = near_activation.astype(jnp.float32) + jnp.einsum(
        "nir,nik->nkr", folded_ahead, down_second, preferred_element_type=jnp.float32
    ).reshape(activation.shape)
    sent = output.astype(jnp.bfloat16)
    last_activation = shifted(sent, "pipe", 1)

    stored = stash[1, 0].reshape(blocks, width, rows)
    behind = front(
        stored, up_first, up_second, down_first,
        to_columns_by_permutes, to_rows_by_permutes,
    )
    grad_step, terms, last_activation = backward(
        stored, near_cotangent, up_first, up_second, down_first, down_second, behind,
        last_activation,
    )
    sent_back = (near_cotangent.astype(jnp.float32) + grad_step).astype(jnp.bfloat16)
    last_cotangent = shifted(sent_back, "pipe", -1)
    activation = last_activation.astype(jnp.float32)
    cotangent = last_cotangent.astype(jnp.float32)
    totals = (
        totals[0] + terms[0],
        totals[1] + terms[1],
        totals[2] + terms[2],
        totals[3] + terms[3],
    )
    return (
        activation[None],
        cotangent[None],
        totals[0][None],
        totals[1][None],
        totals[2][None],
        totals[3][None],
    )


def solution(mesh):
    placed = (
        P("pipe", "tensor", None),
        P(None, "pipe", "tensor", None),
        P("pipe", "tensor", None),
        P("pipe", "tensor", None, None),
        P("pipe", "tensor", None, None),
        P("pipe", "tensor", None, None),
        P("pipe", "tensor", None, None),
    )
    return jax.shard_map(
        body,
        mesh=mesh,
        in_specs=placed,
        out_specs=(
            P("pipe", "tensor", None),
            P("pipe", "tensor", None),
            P("pipe", "tensor", None, None),
            P("pipe", "tensor", None, None),
            P("pipe", "tensor", None, None),
            P("pipe", "tensor", None, None),
        ),
        check_vma=False,
    )
```

```python
import jax
import jax.numpy as jnp
from jax import lax
from jax.sharding import PartitionSpec as P


def shifted(value, axis, by):
    count = lax.axis_size(axis)
    return lax.ppermute(value, axis, [(i, (i + by) % count) for i in range(count)])


def smooth(values):
    return jax.nn.gelu(values, approximate=True)


def to_columns(value):
    return to_columns_by_permutes(value)


def to_rows(value):
    return to_rows_by_permutes(value)


def swapped(pieces):
    count = lax.axis_size("tensor")
    me = lax.axis_index("tensor")
    arrived = []
    for shift in range(count):
        piece = lax.dynamic_index_in_dim(pieces, (me + shift) % count, 0, keepdims=False)
        if shift:
            piece = lax.ppermute(
                piece, "tensor", [(i, (i + shift) % count) for i in range(count)]
            )
        arrived.append(piece)
    order = (me - jnp.arange(count)) % count
    return jnp.take(jnp.stack(arrived), order, axis=0)


def to_columns_by_permutes(value):
    count = lax.axis_size("tensor")
    pieces = value.reshape(value.shape[0], count, -1, value.shape[2]).swapaxes(0, 1)
    out = swapped(pieces)
    return out.reshape((-1,) + out.shape[2:])


def to_rows_by_permutes(value):
    count = lax.axis_size("tensor")
    out = swapped(value.reshape((count, -1) + value.shape[1:]))
    out = out.swapaxes(0, 1)
    return out.reshape(out.shape[0], -1, out.shape[3])


def front(narrow_in, first_up, second_up, first_down, columns=None, rows=None):
    columns = columns or to_columns
    rows = rows or to_rows
    first_out = jnp.einsum(
        "njr,nji->nir", narrow_in, first_up, preferred_element_type=jnp.float32
    ).astype(jnp.bfloat16)
    spread = columns(first_out)
    hidden_pre = jnp.einsum("nir,inf->ifr", spread, second_up, preferred_element_type=jnp.float32)
    hidden = smooth(hidden_pre).astype(jnp.bfloat16)
    local_fold = jnp.einsum(
        "ifr,inf->nir", hidden, first_down, preferred_element_type=jnp.float32
    ).astype(jnp.bfloat16)
    folded = rows(local_fold)
    return (spread, hidden_pre, hidden, folded)


def backward(narrow_in, cotangent, first_up, second_up, first_down, second_down, parts, held=None):
    spread, hidden_pre, hidden, folded = parts
    narrow_grad = cotangent.astype(jnp.bfloat16).reshape(narrow_in.shape)
    grad_second_down = jnp.einsum(
        "nir,nkr->nik", folded, narrow_grad, preferred_element_type=jnp.float32
    )
    local_grad = jnp.einsum(
        "nkr,nik->nir", narrow_grad, second_down, preferred_element_type=jnp.float32
    ).astype(jnp.bfloat16)
    grad_folded = to_columns(local_grad)
    grad_first_down = jnp.einsum(
        "ifr,nir->inf", hidden, grad_folded, preferred_element_type=jnp.float32
    )
    grad_hidden = jnp.einsum(
        "nir,inf->ifr", grad_folded, first_down, preferred_element_type=jnp.float32
    )
    smooth_back = jax.vjp(smooth, hidden_pre)[1]
    grad_pre = smooth_back(grad_hidden)[0].astype(jnp.bfloat16)
    grad_second_up = jnp.einsum(
        "nir,ifr->inf", spread, grad_pre, preferred_element_type=jnp.float32
    )
    column_grad = jnp.einsum(
        "ifr,inf->nir", grad_pre, second_up, preferred_element_type=jnp.float32
    ).astype(jnp.bfloat16)
    grad_first = to_rows(column_grad)
    if held is not None:
        grad_first, held = lax.optimization_barrier((grad_first, held))
    grad_first_up = jnp.einsum(
        "njr,nir->nji", narrow_in, grad_first, preferred_element_type=jnp.float32
    )
    grad_input = jnp.einsum(
        "nir,nji->njr", grad_first, first_up, preferred_element_type=jnp.float32
    ).reshape(cotangent.shape)
    terms = (grad_first_up, grad_second_up, grad_first_down, grad_second_down)
    if held is not None:
        return (grad_input, terms, held)
    return (grad_input, terms)


def body(arriving, stash, grad_in, first_up, second_up, first_down, second_down):
    activation = arriving[0]
    cotangent = grad_in[0]
    up_first = first_up[0]
    up_second = second_up[0]
    down_first = first_down[0]
    down_second = second_down[0]
    blocks = up_first.shape[0]
    width = up_first.shape[1]
    rows = activation.shape[1]
    current = activation.astype(jnp.bfloat16)
    folded_ahead = front(current.reshape(blocks, width, rows), up_first, up_second, down_first)[3]
    output = activation + jnp.einsum(
        "nir,nik->nkr", folded_ahead, down_second, preferred_element_type=jnp.float32
    ).reshape(activation.shape)
    sent = output.astype(jnp.bfloat16)
    near_activation = shifted(sent, "pipe", 1)

    stored = stash[0, 0].reshape(blocks, width, rows)
    behind = front(
        stored, up_first, up_second, down_first,
        to_columns_by_permutes, to_rows_by_permutes,
    )
    grad_step, totals = backward(
        stored, cotangent, up_first, up_second, down_first, down_second, behind
    )
    sent_back = (cotangent + grad_step).astype(jnp.bfloat16)
    near_activation, sent_back = lax.optimization_barrier((near_activation, sent_back))
    near_cotangent = shifted(sent_back, "pipe", -1)

    folded_ahead = front(near_activation.reshape(blocks, width, rows), up_first, up_second, down_first)[3]
    output = near_activation.astype(jnp.float32) + jnp.einsum(
        "nir,nik->nkr", folded_ahead, down_second, preferred_element_type=jnp.float32
    ).reshape(activation.shape)
    sent = output.astype(jnp.bfloat16)
    last_activation = shifted(sent, "pipe", 1)

    stored = stash[1, 0].reshape(blocks, width, rows)
    behind = front(
        stored, up_first, up_second, down_first,
        to_columns_by_permutes, to_rows_by_permutes,
    )
    grad_step, terms, last_activation = backward(
        stored, near_cotangent, up_first, up_second, down_first, down_second, behind,
        last_activation,
    )
    sent_back = (near_cotangent.astype(jnp.float32) + grad_step).astype(jnp.bfloat16)
    last_cotangent = shifted(sent_back, "pipe", -1)
    activation = last_activation.astype(jnp.float32)
    cotangent = last_cotangent.astype(jnp.float32)
    totals = (
        totals[0] + terms[0],
        totals[1] + terms[1],
        totals[2] + terms[2],
        totals[3] + terms[3],
    )
    return (
        activation[None],
        cotangent[None],
        totals[0][None],
        totals[1][None],
        totals[2][None],
        totals[3][None],
    )


def solution(mesh):
    placed = (
        P("pipe", "tensor", None),
        P(None, "pipe", "tensor", None),
        P("pipe", "tensor", None),
        P("pipe", "tensor", None, None),
        P("pipe", "tensor", None, None),
        P("pipe", "tensor", None, None),
        P("pipe", "tensor", None, None),
    )
    return jax.shard_map(
        body,
        mesh=mesh,
        in_specs=placed,
        out_specs=(
            P("pipe", "tensor", None),
            P("pipe", "tensor", None),
            P("pipe", "tensor", None, None),
            P("pipe", "tensor", None, None),
            P("pipe", "tensor", None, None),
            P("pipe", "tensor", None, None),
        ),
        check_vma=False,
    )
```

```python
import jax
import jax.numpy as jnp
from jax import lax
from jax.sharding import PartitionSpec as P


def shifted(value, axis, by):
    count = lax.axis_size(axis)
    return lax.ppermute(value, axis, [(i, (i + by) % count) for i in range(count)])


def smooth(values):
    return jax.nn.gelu(values, approximate=True)


def to_columns(value):
    return lax.all_to_all(value, "tensor", split_axis=1, concat_axis=0, tiled=True)


def to_rows(value):
    return lax.all_to_all(value, "tensor", split_axis=0, concat_axis=1, tiled=True)


def swapped(pieces):
    count = lax.axis_size("tensor")
    me = lax.axis_index("tensor")
    arrived = []
    for shift in range(count):
        piece = lax.dynamic_index_in_dim(pieces, (me + shift) % count, 0, keepdims=False)
        if shift:
            piece = lax.ppermute(
                piece, "tensor", [(i, (i + shift) % count) for i in range(count)]
            )
        arrived.append(piece)
    order = (me - jnp.arange(count)) % count
    return jnp.take(jnp.stack(arrived), order, axis=0)


def to_columns_by_permutes(value):
    count = lax.axis_size("tensor")
    pieces = value.reshape(value.shape[0], count, -1, value.shape[2]).swapaxes(0, 1)
    out = swapped(pieces)
    return out.reshape((-1,) + out.shape[2:])


def to_rows_by_permutes(value):
    count = lax.axis_size("tensor")
    out = swapped(value.reshape((count, -1) + value.shape[1:]))
    out = out.swapaxes(0, 1)
    return out.reshape(out.shape[0], -1, out.shape[3])


def front(narrow_in, first_up, second_up, first_down, columns=None, rows=None):
    columns = columns or to_columns
    rows = rows or to_rows
    first_out = jnp.einsum(
        "njr,nji->nir", narrow_in, first_up, preferred_element_type=jnp.float32
    ).astype(jnp.bfloat16)
    spread = columns(first_out)
    hidden_pre = jnp.einsum("nir,inf->ifr", spread, second_up, preferred_element_type=jnp.float32)
    hidden = smooth(hidden_pre).astype(jnp.bfloat16)
    local_fold = jnp.einsum(
        "ifr,inf->nir", hidden, first_down, preferred_element_type=jnp.float32
    ).astype(jnp.bfloat16)
    folded = rows(local_fold)
    return (spread, hidden_pre, hidden, folded)


def backward(narrow_in, cotangent, first_up, second_up, first_down, second_down, parts, held=None):
    spread, hidden_pre, hidden, folded = parts
    narrow_grad = cotangent.astype(jnp.bfloat16).reshape(narrow_in.shape)
    grad_second_down = jnp.einsum(
        "nir,nkr->nik", folded, narrow_grad, preferred_element_type=jnp.float32
    )
    local_grad = jnp.einsum(
        "nkr,nik->nir", narrow_grad, second_down, preferred_element_type=jnp.float32
    ).astype(jnp.bfloat16)
    grad_folded = to_columns(local_grad)
    grad_first_down = jnp.einsum(
        "ifr,nir->inf", hidden, grad_folded, preferred_element_type=jnp.float32
    )
    grad_hidden = jnp.einsum(
        "nir,inf->ifr", grad_folded, first_down, preferred_element_type=jnp.float32
    )
    smooth_back = jax.vjp(smooth, hidden_pre)[1]
    grad_pre = smooth_back(grad_hidden)[0].astype(jnp.bfloat16)
    grad_second_up = jnp.einsum(
        "nir,ifr->inf", spread, grad_pre, preferred_element_type=jnp.float32
    )
    column_grad = jnp.einsum(
        "ifr,inf->nir", grad_pre, second_up, preferred_element_type=jnp.float32
    ).astype(jnp.bfloat16)
    grad_first = to_rows(column_grad)
    if held is not None:
        grad_first, held = lax.optimization_barrier((grad_first, held))
    grad_first_up = jnp.einsum(
        "njr,nir->nji", narrow_in, grad_first, preferred_element_type=jnp.float32
    )
    grad_input = jnp.einsum(
        "nir,nji->njr", grad_first, first_up, preferred_element_type=jnp.float32
    ).reshape(cotangent.shape)
    terms = (grad_first_up, grad_second_up, grad_first_down, grad_second_down)
    if held is not None:
        return (grad_input, terms, held)
    return (grad_input, terms)


def body(arriving, stash, grad_in, first_up, second_up, first_down, second_down):
    activation = arriving[0]
    cotangent = grad_in[0]
    up_first = first_up[0]
    up_second = second_up[0]
    down_first = first_down[0]
    down_second = second_down[0]
    blocks = up_first.shape[0]
    width = up_first.shape[1]
    rows = activation.shape[1]
    current = activation.astype(jnp.bfloat16)
    folded_ahead = front(current.reshape(blocks, width, rows), up_first, up_second, down_first)[3]
    output = activation + jnp.einsum(
        "nir,nik->nkr", folded_ahead, down_second, preferred_element_type=jnp.float32
    ).reshape(activation.shape)
    sent = output.astype(jnp.bfloat16)
    near_activation = shifted(sent, "pipe", 1)

    stored = stash[0, 0].reshape(blocks, width, rows)
    behind = front(stored, up_first, up_second, down_first)
    grad_step, totals = backward(
        stored, cotangent, up_first, up_second, down_first, down_second, behind
    )
    sent_back = (cotangent + grad_step).astype(jnp.bfloat16)
    near_activation, sent_back = lax.optimization_barrier((near_activation, sent_back))
    near_cotangent = shifted(sent_back, "pipe", -1)

    folded_ahead = front(near_activation.reshape(blocks, width, rows), up_first, up_second, down_first)[3]
    output = near_activation.astype(jnp.float32) + jnp.einsum(
        "nir,nik->nkr", folded_ahead, down_second, preferred_element_type=jnp.float32
    ).reshape(activation.shape)
    sent = output.astype(jnp.bfloat16)
    last_activation = shifted(sent, "pipe", 1)

    stored = stash[1, 0].reshape(blocks, width, rows)
    behind = front(
        stored, up_first, up_second, down_first,
        to_columns_by_permutes, to_rows_by_permutes,
    )
    grad_step, terms, last_activation = backward(
        stored, near_cotangent, up_first, up_second, down_first, down_second, behind,
        last_activation,
    )
    sent_back = (near_cotangent.astype(jnp.float32) + grad_step).astype(jnp.bfloat16)
    last_cotangent = shifted(sent_back, "pipe", -1)
    activation = last_activation.astype(jnp.float32)
    cotangent = last_cotangent.astype(jnp.float32)
    totals = (
        totals[0] + terms[0],
        totals[1] + terms[1],
        totals[2] + terms[2],
        totals[3] + terms[3],
    )
    return (
        activation[None],
        cotangent[None],
        totals[0][None],
        totals[1][None],
        totals[2][None],
        totals[3][None],
    )


def solution(mesh):
    placed = (
        P("pipe", "tensor", None),
        P(None, "pipe", "tensor", None),
        P("pipe", "tensor", None),
        P("pipe", "tensor", None, None),
        P("pipe", "tensor", None, None),
        P("pipe", "tensor", None, None),
        P("pipe", "tensor", None, None),
    )
    return jax.shard_map(
        body,
        mesh=mesh,
        in_specs=placed,
        out_specs=(
            P("pipe", "tensor", None),
            P("pipe", "tensor", None),
            P("pipe", "tensor", None, None),
            P("pipe", "tensor", None, None),
            P("pipe", "tensor", None, None),
            P("pipe", "tensor", None, None),
        ),
        check_vma=False,
    )
```

```python
import jax
import jax.numpy as jnp
from jax import lax
from jax.sharding import PartitionSpec as P


def shifted(value, axis, by):
    count = lax.axis_size(axis)
    return lax.ppermute(value, axis, [(i, (i + by) % count) for i in range(count)])


def smooth(values):
    return jax.nn.gelu(values, approximate=True)


def to_columns(value):
    return lax.all_to_all(value, "tensor", split_axis=1, concat_axis=0, tiled=True)


def to_rows(value):
    return lax.all_to_all(value, "tensor", split_axis=0, concat_axis=1, tiled=True)


def swapped(pieces):
    count = lax.axis_size("tensor")
    me = lax.axis_index("tensor")
    arrived = []
    for shift in range(count):
        piece = lax.dynamic_index_in_dim(pieces, (me + shift) % count, 0, keepdims=False)
        if shift:
            piece = lax.ppermute(
                piece, "tensor", [(i, (i + shift) % count) for i in range(count)]
            )
        arrived.append(piece)
    order = (me - jnp.arange(count)) % count
    return jnp.take(jnp.stack(arrived), order, axis=0)


def to_columns_by_permutes(value):
    count = lax.axis_size("tensor")
    pieces = value.reshape(value.shape[0], count, -1, value.shape[2]).swapaxes(0, 1)
    out = swapped(pieces)
    return out.reshape((-1,) + out.shape[2:])


def to_rows_by_permutes(value):
    count = lax.axis_size("tensor")
    out = swapped(value.reshape((count, -1) + value.shape[1:]))
    out = out.swapaxes(0, 1)
    return out.reshape(out.shape[0], -1, out.shape[3])


def front(narrow_in, first_up, second_up, first_down, columns=None, rows=None):
    columns = columns or to_columns
    rows = rows or to_rows
    first_out = jnp.einsum(
        "njr,nji->nir", narrow_in, first_up, preferred_element_type=jnp.float32
    ).astype(jnp.bfloat16)
    spread = columns(first_out)
    hidden_pre = jnp.einsum("nir,inf->ifr", spread, second_up, preferred_element_type=jnp.float32)
    hidden = smooth(hidden_pre).astype(jnp.bfloat16)
    local_fold = jnp.einsum(
        "ifr,inf->nir", hidden, first_down, preferred_element_type=jnp.float32
    ).astype(jnp.bfloat16)
    folded = rows(local_fold)
    return (spread, hidden_pre, hidden, folded)


def backward(narrow_in, cotangent, first_up, second_up, first_down, second_down, parts, held=None):
    spread, hidden_pre, hidden, folded = parts
    narrow_grad = cotangent.astype(jnp.bfloat16).reshape(narrow_in.shape)
    grad_second_down = jnp.einsum(
        "nir,nkr->nik", folded, narrow_grad, preferred_element_type=jnp.float32
    )
    local_grad = jnp.einsum(
        "nkr,nik->nir", narrow_grad, second_down, preferred_element_type=jnp.float32
    ).astype(jnp.bfloat16)
    grad_folded = to_columns(local_grad)
    grad_first_down = jnp.einsum(
        "ifr,nir->inf", hidden, grad_folded, preferred_element_type=jnp.float32
    )
    grad_hidden = jnp.einsum(
        "nir,inf->ifr", grad_folded, first_down, preferred_element_type=jnp.float32
    )
    smooth_back = jax.vjp(smooth, hidden_pre)[1]
    grad_pre = smooth_back(grad_hidden)[0].astype(jnp.bfloat16)
    grad_second_up = jnp.einsum(
        "nir,ifr->inf", spread, grad_pre, preferred_element_type=jnp.float32
    )
    column_grad = jnp.einsum(
        "ifr,inf->nir", grad_pre, second_up, preferred_element_type=jnp.float32
    ).astype(jnp.bfloat16)
    grad_first = to_rows(column_grad)
    if held is not None:
        grad_first, held = lax.optimization_barrier((grad_first, held))
    grad_first_up = jnp.einsum(
        "njr,nir->nji", narrow_in, grad_first, preferred_element_type=jnp.float32
    )
    grad_input = jnp.einsum(
        "nir,nji->njr", grad_first, first_up, preferred_element_type=jnp.float32
    ).reshape(cotangent.shape)
    terms = (grad_first_up, grad_second_up, grad_first_down, grad_second_down)
    if held is not None:
        return (grad_input, terms, held)
    return (grad_input, terms)


def body(arriving, stash, grad_in, first_up, second_up, first_down, second_down):
    activation = arriving[0]
    cotangent = grad_in[0]
    up_first = first_up[0]
    up_second = second_up[0]
    down_first = first_down[0]
    down_second = second_down[0]
    blocks = up_first.shape[0]
    width = up_first.shape[1]
    rows = activation.shape[1]
    current = activation.astype(jnp.bfloat16)
    folded_ahead = front(current.reshape(blocks, width, rows), up_first, up_second, down_first)[3]
    output = activation + jnp.einsum(
        "nir,nik->nkr", folded_ahead, down_second, preferred_element_type=jnp.float32
    ).reshape(activation.shape)
    sent = output.astype(jnp.bfloat16)
    near_activation = shifted(sent, "pipe", 1)

    stored = stash[0, 0].reshape(blocks, width, rows)
    behind = front(
        stored, up_first, up_second, down_first,
        to_columns_by_permutes, to_rows_by_permutes,
    )
    grad_step, totals = backward(
        stored, cotangent, up_first, up_second, down_first, down_second, behind
    )
    sent_back = (cotangent + grad_step).astype(jnp.bfloat16)
    near_activation, sent_back = lax.optimization_barrier((near_activation, sent_back))
    near_cotangent = shifted(sent_back, "pipe", -1)

    folded_ahead = front(near_activation.reshape(blocks, width, rows), up_first, up_second, down_first)[3]
    output = near_activation.astype(jnp.float32) + jnp.einsum(
        "nir,nik->nkr", folded_ahead, down_second, preferred_element_type=jnp.float32
    ).reshape(activation.shape)
    sent = output.astype(jnp.bfloat16)
    last_activation = shifted(sent, "pipe", 1)

    stored = stash[1, 0].reshape(blocks, width, rows)
    behind = front(stored, up_first, up_second, down_first)
    grad_step, terms, last_activation = backward(
        stored, near_cotangent, up_first, up_second, down_first, down_second, behind,
        last_activation,
    )
    sent_back = (near_cotangent.astype(jnp.float32) + grad_step).astype(jnp.bfloat16)
    last_cotangent = shifted(sent_back, "pipe", -1)
    activation = last_activation.astype(jnp.float32)
    cotangent = last_cotangent.astype(jnp.float32)
    totals = (
        totals[0] + terms[0],
        totals[1] + terms[1],
        totals[2] + terms[2],
        totals[3] + terms[3],
    )
    return (
        activation[None],
        cotangent[None],
        totals[0][None],
        totals[1][None],
        totals[2][None],
        totals[3][None],
    )


def solution(mesh):
    placed = (
        P("pipe", "tensor", None),
        P(None, "pipe", "tensor", None),
        P("pipe", "tensor", None),
        P("pipe", "tensor", None, None),
        P("pipe", "tensor", None, None),
        P("pipe", "tensor", None, None),
        P("pipe", "tensor", None, None),
    )
    return jax.shard_map(
        body,
        mesh=mesh,
        in_specs=placed,
        out_specs=(
            P("pipe", "tensor", None),
            P("pipe", "tensor", None),
            P("pipe", "tensor", None, None),
            P("pipe", "tensor", None, None),
            P("pipe", "tensor", None, None),
            P("pipe", "tensor", None, None),
        ),
        check_vma=False,
    )
```
